32 devices in a mesh: chan: 2 (over core), sky: 16 (over z, y, x).
Axes of the slice: x: 2, y: 2, z: 4, core: 2. Of those that a mesh axis runs over, the one named last changes fastest.
Arguments:
- dirty: bfloat16 [4, 256, 2048], P('chan', None, 'sky'), may hold values from -6 to 6
- model: float32 [4, 256, 2048], P(None, 'chan', 'sky'), may hold values from -3 to 3
- spectral: float32 [4, 4], replicated, may hold values from 0.25 to 1.5
- psf_rows: float32 [4, 4, 129], replicated, may hold values from -0.5 to 0.5
- psf_cols: float32 [4, 4, 129], replicated, may hold values from -0.5 to 0.5
- strip_width: int32 [16], replicated, may hold values from 128 to 128, as said below
Outputs:
- residual: bfloat16 [4, 256, 2048], P('chan', None, 'sky')
- model_new: float32 [4, 256, 2048], P(None, 'chan', 'sky')
The draws below stay inside these ranges and needn't reach their ends.
Inputs may be any that keep to these rules, and one draw needn't show every extreme that they name: `strip_width`: every strip has between 128 and 128 live columns, left-aligned in its slot; some strip has exactly 128 and some strip exactly 128.
All inputs are finite; a program needn't handle non-finite values.
Results may differ from the reference program's by a relative error of at most 0.0064.
Values may be sent and summed in bfloat16 or wider, within the bound.
No kernel may reach another device: no remote copies, remote signals or barrier semaphores. Data moves between devices by JAX's collectives and lax.ppermute only.
A program may use at most 64 MiB of HBM per device.

```python
import jax
import jax.numpy as jnp
from jax import lax

ROWS = 256
SLOT = 128
BASIS = 4
RANK = 4
TAPS = 129
HALF = 64
MINW = 128
NCHAN = 4
COLS = 2048
N_SKY = 16


def draw_strip_width(key, part):
    first_key, second_key = jax.random.split(jax.random.fold_in(key, 17))
    widths = jax.random.randint(first_key, (N_SKY,), MINW, SLOT + 1, dtype=jnp.int32)
    order = jax.random.permutation(second_key, N_SKY)
    widths = widths.at[order[0]].set(SLOT)
    widths = widths.at[order[1]].set(MINW)
    return widths.astype(jnp.int32)


def shard_levels(stream_key, shape, shards, smallest, high):
    def one(position, parts):
        draws = jax.random.uniform(jax.random.fold_in(jax.random.fold_in(stream_key, 6), position), (parts,), jnp.float32, smallest / len(shards), high / len(shards))
        return jnp.repeat(jnp.exp(draws), shape[position] // parts).reshape((-1,) + (1,) * (len(shape) - position - 1))

    loudness = one(*shards[0])
    for cut in shards[1:]:
        loudness = loudness * one(*cut)
    return loudness


def centred(stream_key, extent, scale, limit, pieces=(), kind=jnp.bfloat16):
    values = jax.random.normal(stream_key, extent, jnp.float32) * scale
    if len(pieces) > 0:
        values = shard_levels(stream_key, extent, pieces, -0.22, 0.18) * values
    return jnp.clip(values, min=-limit, max=limit).astype(kind)


def setup_inputs(seed: int = 0) -> dict:
    splits = jax.random.split(jax.random.key(seed), 7)
    dirty = centred(splits[0], (NCHAN, ROWS, COLS), 1.0, 6.0, ((0, 2), (2, 16)))
    model = centred(splits[1], (BASIS, ROWS, COLS), 0.5, 3.0, ((1, 2), (2, 16)), jnp.float32)
    spectral = jnp.clip(jax.random.uniform(splits[2], (NCHAN, BASIS), jnp.float32, 0.25, 1.5), 0.25, 1.5)
    psf_rows = centred(splits[3], (NCHAN, RANK, TAPS), TAPS ** -0.5, 0.5, (), jnp.float32)
    psf_cols = centred(splits[4], (NCHAN, RANK, TAPS), TAPS ** -0.5, 0.5, (), jnp.float32)
    strip_width = draw_strip_width(jax.random.fold_in(splits[6], 71), 0)
    return {"dirty": dirty, "model": model, "spectral": spectral, "psf_rows": psf_rows, "psf_cols": psf_cols, "strip_width": strip_width}


def conv_pass(lhs, taps):
    return lax.conv_general_dilated(lhs, taps, (1,), ((HALF, HALF),), dimension_numbers=("NCH", "OIH", "NCH"), precision=lax.Precision.HIGHEST)


def apply_psf(field, row_taps, col_taps):
    col_pass = conv_pass(field.astype(jnp.float32)[:, None, :], col_taps.astype(jnp.float32)[:, None, :])
    col_pass = col_pass.astype(jnp.bfloat16)
    row_input = jnp.transpose(col_pass, (2, 1, 0)).astype(jnp.float32)
    outcome = conv_pass(row_input, row_taps.astype(jnp.float32)[None, :, :])
    return jnp.transpose(outcome[:, 0, :], (1, 0))


def reference(dirty, model, spectral, psf_rows, psf_cols, strip_width):
    slot_pos = jnp.arange(SLOT, dtype=jnp.int32)
    live_mask = (slot_pos[None, :] < strip_width[:, None]).reshape(COLS)
    offsets = (jnp.cumsum(strip_width) - strip_width).astype(jnp.int32)
    compact_index = (offsets[:, None] + slot_pos[None, :]).reshape(COLS)
    compact_index = jnp.where(live_mask, compact_index, COLS).astype(jnp.int32)
    fetch_index = jnp.minimum(compact_index, COLS - 1).astype(jnp.int32)

    def to_compact(field):
        return jnp.zeros((ROWS, COLS), field.dtype).at[:, compact_index].set(field, mode="drop")

    def from_compact(field):
        return jnp.where(live_mask[None, :], field[:, fetch_index], jnp.zeros((), field.dtype))

    row_bf = psf_rows.astype(jnp.bfloat16)
    col_bf = psf_cols.astype(jnp.bfloat16)

    def channel_step(grad_acc, inputs):
        dirty_chan, spec_chan, row_taps, col_taps = inputs
        sky_image = spec_chan[0] * model[0]
        for basis_idx in range(1, BASIS):
            sky_image = sky_image + spec_chan[basis_idx] * model[basis_idx]
        sky_image = jnp.where(live_mask[None, :], sky_image, 0.0).astype(jnp.bfloat16)
        predicted = from_compact(apply_psf(to_compact(sky_image), row_taps, col_taps))
        resid_chan = jnp.where(live_mask[None, :], dirty_chan.astype(jnp.float32) - predicted, 0.0).astype(jnp.bfloat16)
        grad_chan = from_compact(apply_psf(to_compact(resid_chan), row_taps[:, ::-1], col_taps[:, ::-1]))
        grad_acc = grad_acc + spec_chan[:, None, None] * grad_chan[None, :, :]
        return grad_acc, resid_chan

    grad_init = jnp.zeros((BASIS, ROWS, COLS), jnp.float32)
    grad_total, residual = lax.scan(channel_step, grad_init, (dirty, spectral, row_bf, col_bf))
    gram_rows = jnp.einsum("crt,cst->crs", psf_rows, psf_rows, precision=lax.Precision.HIGHEST)
    gram_cols = jnp.einsum("crt,cst->crs", psf_cols, psf_cols, precision=lax.Precision.HIGHEST)
    energy = jnp.sum(gram_rows * gram_cols, axis=(1, 2))
    curvature = jnp.sum(spectral * spectral * energy[:, None], axis=0)
    model_new = jnp.where(live_mask[None, None, :], model + grad_total / curvature[:, None, None], 0.0)
    return residual, model_new
```

```python
import functools

import jax
import jax.numpy as jnp
from jax import lax
from jax.experimental import pallas as pl
from jax.experimental.pallas import tpu as pltpu
from jax.sharding import PartitionSpec as P

TAPS = 129
HALF = (TAPS - 1) // 2
LANES = 512


def from_behind(value, axis, steps):
    count = lax.axis_size(axis)
    first, last = (max(0, -steps), min(count, count - steps))
    return lax.ppermute(value, axis, [(source, source + steps) for source in range(first, last)])


def tap_table(psf_rows, psf_cols, first_chan, local_chans):
    rows = lax.dynamic_slice_in_dim(psf_rows, first_chan, local_chans, 0)
    cols = lax.dynamic_slice_in_dim(psf_cols, first_chan, local_chans, 0)
    rows = rows.astype(jnp.bfloat16).astype(jnp.float32)
    cols = cols.astype(jnp.bfloat16).astype(jnp.float32)
    kinds = jnp.stack([cols[..., ::-1], cols, rows, rows[..., ::-1]], axis=1)
    kinds = jnp.pad(kinds, ((0, 0), (0, 0), (0, 0), (0, LANES - TAPS)))
    return kinds.reshape(local_chans, -1, LANES)


def col_band(w, slot):
    ext = slot + 2 * HALF
    spread = jnp.broadcast_to(w[:, :ext], (ext, ext))
    return pltpu.roll(spread, ext - 2 * HALF, 1, stride=1, stride_axis=0)[:, :slot]


def row_band(w, rows):
    spread = jnp.broadcast_to(w, (rows, LANES))
    return pltpu.roll(spread, LANES - HALF, 1, stride=1, stride_axis=0)[:, :rows]


def psf_pass(tab, base, left, centre, right, rank_count):
    rows, slot = centre.shape
    bands = [
        col_band(tab[base + r : base + r + 1, :], slot).astype(jnp.bfloat16)
        for r in range(rank_count)
    ]
    band = jnp.concatenate(bands, axis=1)
    col_pass = (
        jnp.dot(left, band[:HALF], preferred_element_type=jnp.float32)
        + jnp.dot(centre, band[HALF : HALF + slot], preferred_element_type=jnp.float32)
        + jnp.dot(right, band[HALF + slot :], preferred_element_type=jnp.float32)
    ).astype(jnp.bfloat16)
    total = None
    for r in range(rank_count):
        rb = row_band(tab[base + 2 * rank_count + r : base + 2 * rank_count + r + 1, :], rows)
        part = jnp.dot(
            rb.astype(jnp.bfloat16),
            col_pass[:, r * slot : (r + 1) * slot],
            preferred_element_type=jnp.float32,
        )
        total = part if total is None else total + part
    return total


def forward_kernel(rank_count, tab_ref, xl_ref, xc_ref, xr_ref, dirty_ref, res_ref):
    for c in range(xc_ref.shape[0]):
        tab = tab_ref[c]
        pred = psf_pass(tab, 0, xl_ref[c], xc_ref[c], xr_ref[c], rank_count)
        res_ref[c] = (dirty_ref[c].astype(jnp.float32) - pred).astype(res_ref.dtype)


def adjoint_kernel(rank_count, spec_ref, tab_ref, rl_ref, rc_ref, rr_ref, out_ref):
    basis = out_ref.shape[0]
    for c in range(rc_ref.shape[0]):
        tab = tab_ref[c]
        grad_chan = psf_pass(tab, rank_count, rl_ref[c], rc_ref[c], rr_ref[c], rank_count)
        for b in range(basis):
            term = spec_ref[c, b] * grad_chan
            if c == 0:
                out_ref[b] = term
            else:
                out_ref[b] = out_ref[b] + term


def vmem_spec():
    return pl.BlockSpec(memory_space=pltpu.VMEM)


def body(dirty, model, spectral, psf_rows, psf_cols, strip_width):
    local_chans, row_count, slot_width = dirty.shape
    basis = model.shape[0]
    rank_count = psf_rows.shape[1]
    chan_count = lax.axis_size("chan")
    first_chan = lax.axis_index("chan") * local_chans

    image_rows = spectral[:, 0][:, None, None] * model[0][None]
    for basis_idx in range(1, basis):
        image_rows = image_rows + spectral[:, basis_idx][:, None, None] * model[basis_idx][None]
    image_rows = image_rows.astype(jnp.bfloat16)
    image = lax.all_to_all(image_rows, "chan", 0, 1, tiled=True)

    tab = tap_table(psf_rows, psf_cols, first_chan, local_chans)
    spec_local = lax.dynamic_slice_in_dim(spectral, first_chan, local_chans, 0)

    xl = from_behind(image[:, :, slot_width - HALF :], "sky", 1)
    xr = from_behind(image[:, :, :HALF], "sky", -1)
    residual = pl.pallas_call(
        functools.partial(forward_kernel, rank_count),
        out_shape=jax.ShapeDtypeStruct(dirty.shape, jnp.bfloat16),
        in_specs=[vmem_spec()] * 5,
        out_specs=vmem_spec(),
    )(tab, xl, image, xr, dirty)

    rl = from_behind(residual[:, :, slot_width - HALF :], "sky", 1)
    rr = from_behind(residual[:, :, :HALF], "sky", -1)
    partial_value = pl.pallas_call(
        functools.partial(adjoint_kernel, rank_count),
        out_shape=jax.ShapeDtypeStruct((basis, row_count, slot_width), jnp.float32),
        in_specs=[pl.BlockSpec(memory_space=pltpu.SMEM)] + [vmem_spec()] * 4,
        out_specs=vmem_spec(),
    )(spec_local, tab, rl, residual, rr)

    pieces = lax.all_to_all(partial_value, "chan", 1, 0, tiled=True)
    grad_share = pieces.reshape(chan_count, basis, row_count // chan_count, slot_width).sum(0)

    gram_rows = jnp.einsum("crt,cst->crs", psf_rows, psf_rows, precision=lax.Precision.HIGHEST)
    gram_cols = jnp.einsum("crt,cst->crs", psf_cols, psf_cols, precision=lax.Precision.HIGHEST)
    energy = jnp.sum(gram_rows * gram_cols, axis=(1, 2))
    curvature = jnp.sum(spectral * spectral * energy[:, None], axis=0)
    model_new = model + grad_share / curvature[:, None, None]
    return (residual, model_new)


def solution(mesh):
    placed = (P("chan", None, "sky"), P(None, "chan", "sky"), P(), P(), P(), P())
    return jax.shard_map(
        body,
        mesh=mesh,
        in_specs=placed,
        out_specs=(P("chan", None, "sky"), P(None, "chan", "sky")),
        check_vma=False,
    )
```

```python
import functools

import jax
import jax.numpy as jnp
from jax import lax
from jax.experimental import pallas as pl
from jax.experimental.pallas import tpu as pltpu
from jax.sharding import PartitionSpec as P

TAPS = 129
HALF = (TAPS - 1) // 2
LANES = 512


def from_behind(value, axis, steps):
    count = lax.axis_size(axis)
    first, last = (max(0, -steps), min(count, count - steps))
    return lax.ppermute(value, axis, [(source, source + steps) for source in range(first, last)])


def tap_table(psf_rows, psf_cols, first_chan, local_chans):
    rows = lax.dynamic_slice_in_dim(psf_rows, first_chan, local_chans, 0)
    cols = lax.dynamic_slice_in_dim(psf_cols, first_chan, local_chans, 0)
    rows = rows.astype(jnp.bfloat16).astype(jnp.float32)
    cols = cols.astype(jnp.bfloat16).astype(jnp.float32)
    kinds = jnp.stack([cols[..., ::-1], cols, rows, rows[..., ::-1]], axis=1)
    kinds = jnp.pad(kinds, ((0, 0), (0, 0), (0, 0), (0, LANES - TAPS)))
    return kinds.reshape(local_chans, -1, LANES)


def col_band(w, slot):
    ext = slot + 2 * HALF
    spread = jnp.broadcast_to(w[:, :ext], (ext, ext))
    return pltpu.roll(spread, ext - 2 * HALF, 1, stride=1, stride_axis=0)[:, :slot]


def row_band(w, rows):
    spread = jnp.broadcast_to(w, (rows, LANES))
    return pltpu.roll(spread, LANES - HALF, 1, stride=1, stride_axis=0)[:, :rows]


def band_kernel(rank_count, slot, tab_ref, colf_ref, rowf_ref, cola_ref, rowa_ref):
    rows = rowf_ref.shape[-1]
    for c in range(tab_ref.shape[0]):
        tab = tab_ref[c]
        for kind, col_ref, row_ref in ((0, colf_ref, rowf_ref), (1, cola_ref, rowa_ref)):
            for r in range(rank_count):
                w = tab[kind * rank_count + r : kind * rank_count + r + 1, :]
                col_ref[c, :, r * slot : (r + 1) * slot] = col_band(w, slot).astype(jnp.bfloat16)
                w = tab[(kind + 2) * rank_count + r : (kind + 2) * rank_count + r + 1, :]
                row_ref[c, r] = row_band(w, rows).astype(jnp.bfloat16)


def row_pass(row_ref, c, col_pass, rank_count, slot):
    total = None
    for r in range(rank_count):
        part = jnp.dot(
            row_ref[c, r], col_pass[:, r * slot : (r + 1) * slot], preferred_element_type=jnp.float32
        )
        total = part if total is None else total + part
    return total


def main_kernel(
    rank_count, spec_ref, edge_ref, colf_ref, rowf_ref, cola_ref, rowa_ref,
    xl_ref, xc_ref, xr_ref, dirty_ref, dl_ref, dr_ref, res_ref, part_ref,
):
    slot = xc_ref.shape[-1]
    pieces, basis, piece_rows, _ = part_ref.shape
    lane = lax.broadcasted_iota(jnp.int32, (xc_ref.shape[1], slot), 1)
    for c in range(xc_ref.shape[0]):
        band = colf_ref[c]
        xl, xc, xr = xl_ref[c], xc_ref[c], xr_ref[c]
        low = (
            jnp.dot(xl, band[:slot], preferred_element_type=jnp.float32)
            + jnp.dot(xc, band[slot:], preferred_element_type=jnp.float32)
        ).astype(jnp.bfloat16)
        high = (
            jnp.dot(xc, band[:slot], preferred_element_type=jnp.float32)
            + jnp.dot(xr, band[slot:], preferred_element_type=jnp.float32)
        ).astype(jnp.bfloat16)
        pred_low = row_pass(rowf_ref, c, low, rank_count, slot)
        pred_high = row_pass(rowf_ref, c, high, rank_count, slot)
        pred_own = pltpu.roll(jnp.where(lane < HALF, pred_high, pred_low), HALF, 1)
        res_own = (dirty_ref[c].astype(jnp.float32) - pred_own).astype(jnp.bfloat16)
        res_ref[c] = res_own
        halo_l = jnp.where(edge_ref[0] > 0, dl_ref[c].astype(jnp.float32) - pred_low[:, :HALF], 0.0)
        pred_right = pltpu.roll(pred_high, slot - HALF, 1)[:, :HALF]
        halo_r = jnp.where(edge_ref[1] > 0, dr_ref[c].astype(jnp.float32) - pred_right, 0.0)
        adj = cola_ref[c]
        col_pass = (
            jnp.dot(halo_l.astype(jnp.bfloat16), adj[:HALF], preferred_element_type=jnp.float32)
            + jnp.dot(res_own, adj[HALF : HALF + slot], preferred_element_type=jnp.float32)
            + jnp.dot(halo_r.astype(jnp.bfloat16), adj[HALF + slot :], preferred_element_type=jnp.float32)
        ).astype(jnp.bfloat16)
        grad_chan = row_pass(rowa_ref, c, col_pass, rank_count, slot)
        for j in range(pieces):
            block = grad_chan[j * piece_rows : (j + 1) * piece_rows]
            for b in range(basis):
                term = spec_ref[c, b] * block
                if c == 0:
                    part_ref[j, b] = term
                else:
                    part_ref[j, b] = part_ref[j, b] + term


def vmem_spec():
    return pl.BlockSpec(memory_space=pltpu.VMEM)


def smem_spec():
    return pl.BlockSpec(memory_space=pltpu.SMEM)


def body(dirty, model, spectral, psf_rows, psf_cols, strip_width):
    local_chans, row_count, slot_width = dirty.shape
    basis = model.shape[0]
    rank_count = psf_rows.shape[1]
    chan_count = lax.axis_size("chan")
    sky_count = lax.axis_size("sky")
    sky_index = lax.axis_index("sky")
    first_chan = lax.axis_index("chan") * local_chans

    dl = from_behind(dirty[:, :, slot_width - HALF :], "sky", 1)
    dr = from_behind(dirty[:, :, :HALF], "sky", -1)

    image_rows = spectral[:, 0][:, None, None] * model[0][None]
    for basis_idx in range(1, basis):
        image_rows = image_rows + spectral[:, basis_idx][:, None, None] * model[basis_idx][None]
    image_rows = image_rows.astype(jnp.bfloat16)
    image = lax.all_to_all(image_rows, "chan", 0, 1, tiled=True)
    xl = from_behind(image, "sky", 1)
    xr = from_behind(image, "sky", -1)

    tab = tap_table(psf_rows, psf_cols, first_chan, local_chans)
    band_shapes = (
        jax.ShapeDtypeStruct((local_chans, slot_width + 2 * HALF, rank_count * slot_width), jnp.bfloat16),
        jax.ShapeDtypeStruct((local_chans, rank_count, row_count, row_count), jnp.bfloat16),
    )
    colf, rowf, cola, rowa = pl.pallas_call(
        functools.partial(band_kernel, rank_count, slot_width),
        out_shape=band_shapes * 2,
        in_specs=[vmem_spec()],
        out_specs=[vmem_spec()] * 4,
    )(tab)

    spec_local = lax.dynamic_slice_in_dim(spectral, first_chan, local_chans, 0)
    edges = jnp.stack([sky_index > 0, sky_index < sky_count - 1]).astype(jnp.int32)
    piece_rows = row_count // chan_count
    residual, partial_value = pl.pallas_call(
        functools.partial(main_kernel, rank_count),
        out_shape=(
            jax.ShapeDtypeStruct(dirty.shape, jnp.bfloat16),
            jax.ShapeDtypeStruct((chan_count, basis, piece_rows, slot_width), jnp.float32),
        ),
        in_specs=[smem_spec()] * 2 + [vmem_spec()] * 10,
        out_specs=[vmem_spec()] * 2,
    )(spec_local, edges, colf, rowf, cola, rowa, xl, image, xr, dirty, dl, dr)

    pieces = lax.all_to_all(partial_value, "chan", 0, 0, tiled=True)
    grad_share = pieces.sum(0)

    gram_rows = jnp.einsum("crt,cst->crs", psf_rows, psf_rows, precision=lax.Precision.HIGHEST)
    gram_cols = jnp.einsum("crt,cst->crs", psf_cols, psf_cols, precision=lax.Precision.HIGHEST)
    energy = jnp.sum(gram_rows * gram_cols, axis=(1, 2))
    curvature = jnp.sum(spectral * spectral * energy[:, None], axis=0)
    model_new = model + grad_share / curvature[:, None, None]
    return (residual, model_new)


def solution(mesh):
    placed = (P("chan", None, "sky"), P(None, "chan", "sky"), P(), P(), P(), P())
    return jax.shard_map(
        body,
        mesh=mesh,
        in_specs=placed,
        out_specs=(P("chan", None, "sky"), P(None, "chan", "sky")),
        check_vma=False,
    )
```

```python
import functools

import jax
import jax.numpy as jnp
from jax import lax
from jax.experimental import pallas as pl
from jax.experimental.pallas import tpu as pltpu
from jax.sharding import PartitionSpec as P

TAPS = 129
HALF = (TAPS - 1) // 2
LANES = 512


def from_behind(value, axis, steps):
    count = lax.axis_size(axis)
    first, last = (max(0, -steps), min(count, count - steps))
    return lax.ppermute(value, axis, [(source, source + steps) for source in range(first, last)])


def col_band(w, slot):
    ext = slot + 2 * HALF
    spread = jnp.broadcast_to(w[:, :ext], (ext, ext))
    return pltpu.roll(spread, ext - 2 * HALF, 1, stride=1, stride_axis=0)[:, :slot]


def row_band(w, rows):
    spread = jnp.broadcast_to(w, (rows, LANES))
    return pltpu.roll(spread, LANES - HALF, 1, stride=1, stride_axis=0)[:, :rows]


def row_pass(row_ref, col_pass, rank_count, slot):
    total = None
    for r in range(rank_count):
        part = jnp.dot(
            row_ref[r], col_pass[:, r * slot : (r + 1) * slot], preferred_element_type=jnp.float32
        )
        total = part if total is None else total + part
    return total


def main_kernel(
    rank_count, local_chans, sky_count, spec_ref, taps_ref, left_ref, xc_ref, right_ref, dirty_ref,
    res_ref, part_ref, colf_ref, rowf_ref, cola_ref, rowa_ref,
):
    slot = xc_ref.shape[-1]
    rows = xc_ref.shape[1]
    pieces, basis, piece_rows, _ = part_ref.shape
    first_chan = lax.axis_index("chan") * local_chans
    sky_index = lax.axis_index("sky")
    lane = lax.broadcasted_iota(jnp.int32, (rows, slot), 1)
    flip = (
        lax.broadcasted_iota(jnp.int32, (LANES // 2, LANES), 0)
        + lax.broadcasted_iota(jnp.int32, (LANES // 2, LANES), 1)
        == TAPS - 1
    ).astype(jnp.bfloat16)
    for c in range(local_chans):
        taps = taps_ref[first_chan + c].astype(jnp.bfloat16)
        rev = jnp.dot(taps[:, : LANES // 2], flip, preferred_element_type=jnp.float32)
        taps = taps.astype(jnp.float32)
        for r in range(rank_count):
            u, v = taps[r : r + 1], taps[rank_count + r : rank_count + r + 1]
            u_rev, v_rev = rev[r : r + 1], rev[rank_count + r : rank_count + r + 1]
            colf_ref[:, r * slot : (r + 1) * slot] = col_band(v_rev, slot).astype(jnp.bfloat16)
            cola_ref[:, r * slot : (r + 1) * slot] = col_band(v, slot).astype(jnp.bfloat16)
            rowf_ref[r] = row_band(u, rows).astype(jnp.bfloat16)
            rowa_ref[r] = row_band(u_rev, rows).astype(jnp.bfloat16)
        band = colf_ref[...]
        xl, xc, xr = left_ref[c, :, :slot], xc_ref[c], right_ref[c, :, :slot]
        low = (
            jnp.dot(xl, band[:slot], preferred_element_type=jnp.float32)
            + jnp.dot(xc, band[slot:], preferred_element_type=jnp.float32)
        ).astype(jnp.bfloat16)
        high = (
            jnp.dot(xc, band[:slot], preferred_element_type=jnp.float32)
            + jnp.dot(xr, band[slot:], preferred_element_type=jnp.float32)
        ).astype(jnp.bfloat16)
        pred_low = row_pass(rowf_ref, low, rank_count, slot)
        pred_high = row_pass(rowf_ref, high, rank_count, slot)
        pred_own = pltpu.roll(jnp.where(lane < HALF, pred_high, pred_low), HALF, 1)
        res_own = (dirty_ref[c].astype(jnp.float32) - pred_own).astype(jnp.bfloat16)
        res_ref[c] = res_own
        dl = left_ref[c, :, slot : slot + HALF].astype(jnp.float32)
        dr = right_ref[c, :, slot : slot + HALF].astype(jnp.float32)
        halo_l = jnp.where(sky_index > 0, dl - pred_low[:, :HALF], 0.0)
        pred_right = pltpu.roll(pred_high, slot - HALF, 1)[:, :HALF]
        halo_r = jnp.where(sky_index < sky_count - 1, dr - pred_right, 0.0)
        adj = cola_ref[...]
        col_pass = (
            jnp.dot(halo_l.astype(jnp.bfloat16), adj[:HALF], preferred_element_type=jnp.float32)
            + jnp.dot(res_own, adj[HALF : HALF + slot], preferred_element_type=jnp.float32)
            + jnp.dot(halo_r.astype(jnp.bfloat16), adj[HALF + slot :], preferred_element_type=jnp.float32)
        ).astype(jnp.bfloat16)
        grad_chan = row_pass(rowa_ref, col_pass, rank_count, slot)
        for j in range(pieces):
            block = grad_chan[j * piece_rows : (j + 1) * piece_rows]
            for b in range(basis):
                term = spec_ref[first_chan + c, b] * block
                if c == 0:
                    part_ref[j, b] = term
                else:
                    part_ref[j, b] = part_ref[j, b] + term


def vmem_spec():
    return pl.BlockSpec(memory_space=pltpu.VMEM)


def smem_spec():
    return pl.BlockSpec(memory_space=pltpu.SMEM)


def body(dirty, model, spectral, psf_rows, psf_cols, strip_width):
    local_chans, row_count, slot_width = dirty.shape
    basis = model.shape[0]
    rank_count = psf_rows.shape[1]
    chan_count = lax.axis_size("chan")
    sky_count = lax.axis_size("sky")

    image_rows = spectral[:, 0][:, None, None] * model[0][None]
    for basis_idx in range(1, basis):
        image_rows = image_rows + spectral[:, basis_idx][:, None, None] * model[basis_idx][None]
    image_rows = image_rows.astype(jnp.bfloat16)
    image = lax.all_to_all(image_rows, "chan", 0, 1, tiled=True)
    to_right = jnp.concatenate([image, dirty[:, :, slot_width - HALF :]], axis=2)
    to_left = jnp.concatenate([image, dirty[:, :, :HALF]], axis=2)
    left = from_behind(to_right, "sky", 1)
    right = from_behind(to_left, "sky", -1)

    taps = jnp.concatenate([psf_rows, psf_cols], axis=1)
    taps = jnp.pad(taps, ((0, 0), (0, 0), (0, LANES - TAPS)))
    piece_rows = row_count // chan_count
    ext = slot_width + 2 * HALF
    residual, partial_value = pl.pallas_call(
        functools.partial(main_kernel, rank_count, local_chans, sky_count),
        out_shape=(
            jax.ShapeDtypeStruct(dirty.shape, jnp.bfloat16),
            jax.ShapeDtypeStruct((chan_count, basis, piece_rows, slot_width), jnp.float32),
        ),
        in_specs=[smem_spec()] + [vmem_spec()] * 5,
        out_specs=[vmem_spec()] * 2,
        scratch_shapes=[
            pltpu.VMEM((ext, rank_count * slot_width), jnp.bfloat16),
            pltpu.VMEM((rank_count, row_count, row_count), jnp.bfloat16),
            pltpu.VMEM((ext, rank_count * slot_width), jnp.bfloat16),
            pltpu.VMEM((rank_count, row_count, row_count), jnp.bfloat16),
        ],
    )(spectral, taps, left, image, right, dirty)

    pieces = lax.all_to_all(partial_value, "chan", 0, 0, tiled=True)
    grad_share = pieces.sum(0)

    gram_rows = jnp.einsum("crt,cst->crs", psf_rows, psf_rows, precision=lax.Precision.HIGHEST)
    gram_cols = jnp.einsum("crt,cst->crs", psf_cols, psf_cols, precision=lax.Precision.HIGHEST)
    energy = jnp.sum(gram_rows * gram_cols, axis=(1, 2))
    curvature = jnp.sum(spectral * spectral * energy[:, None], axis=0)
    model_new = model + grad_share / curvature[:, None, None]
    return (residual, model_new)


def solution(mesh):
    placed = (P("chan", None, "sky"), P(None, "chan", "sky"), P(), P(), P(), P())
    return jax.shard_map(
        body,
        mesh=mesh,
        in_specs=placed,
        out_specs=(P("chan", None, "sky"), P(None, "chan", "sky")),
        check_vma=False,
    )
```

```python
import functools

import jax
import jax.numpy as jnp
from jax import lax
from jax.experimental import pallas as pl
from jax.experimental.pallas import tpu as pltpu
from jax.sharding import PartitionSpec as P

TAPS = 129
HALF = (TAPS - 1) // 2
LANES = 512


def from_behind(value, axis, steps):
    count = lax.axis_size(axis)
    first, last = (max(0, -steps), min(count, count - steps))
    return lax.ppermute(value, axis, [(source, source + steps) for source in range(first, last)])


def col_band(w, slot):
    ext = slot + 2 * HALF
    spread = jnp.broadcast_to(w[:, :ext], (ext, ext))
    return pltpu.roll(spread, ext - 2 * HALF, 1, stride=1, stride_axis=0)[:, :slot]


def row_band(w, rows):
    spread = jnp.broadcast_to(w, (rows, LANES))
    return pltpu.roll(spread, LANES - HALF, 1, stride=1, stride_axis=0)[:, :rows]


def row_pass(row_ref, col_pass, rank_count, slot):
    total = None
    for r in range(rank_count):
        part = jnp.dot(
            row_ref[r], col_pass[:, r * slot : (r + 1) * slot], preferred_element_type=jnp.float32
        )
        total = part if total is None else total + part
    return total


def unpack_cols(packed):
    return jnp.concatenate([packed[:, :HALF], pltpu.roll(packed, HALF, 1)[:, :HALF]], axis=0)


def main_kernel(
    rank_count, local_chans, sky_count, spec_ref, taps_ref, left_ref, xc_ref, right_ref, dirty_ref,
    res_ref, part_ref, colf_ref, rowf_ref, cola_ref, rowa_ref,
):
    slot = xc_ref.shape[-1]
    rows = xc_ref.shape[1]
    pieces, basis, piece_rows, _ = part_ref.shape
    first_chan = lax.axis_index("chan") * local_chans
    sky_index = lax.axis_index("sky")
    lane = lax.broadcasted_iota(jnp.int32, (rows, slot), 1)
    flip = (
        lax.broadcasted_iota(jnp.int32, (LANES // 2, LANES), 0)
        + lax.broadcasted_iota(jnp.int32, (LANES // 2, LANES), 1)
        == TAPS - 1
    ).astype(jnp.bfloat16)
    for c in range(local_chans):
        taps = taps_ref[first_chan + c].astype(jnp.bfloat16)
        rev = jnp.dot(taps[:, : LANES // 2], flip, preferred_element_type=jnp.float32)
        taps = taps.astype(jnp.float32)
        for r in range(rank_count):
            u, v = taps[r : r + 1], taps[rank_count + r : rank_count + r + 1]
            u_rev, v_rev = rev[r : r + 1], rev[rank_count + r : rank_count + r + 1]
            colf_ref[:, r * slot : (r + 1) * slot] = col_band(v_rev, slot).astype(jnp.bfloat16)
            cola_ref[:, r * slot : (r + 1) * slot] = col_band(v, slot).astype(jnp.bfloat16)
            rowf_ref[r] = row_band(u, rows).astype(jnp.bfloat16)
            rowa_ref[r] = row_band(u_rev, rows).astype(jnp.bfloat16)
        band = colf_ref[...]
        xl, xc, xr = left_ref[c, :rows], xc_ref[c], right_ref[c, :rows]
        low = (
            jnp.dot(xl, band[:slot], preferred_element_type=jnp.float32)
            + jnp.dot(xc, band[slot:], preferred_element_type=jnp.float32)
        ).astype(jnp.bfloat16)
        high = (
            jnp.dot(xc, band[:slot], preferred_element_type=jnp.float32)
            + jnp.dot(xr, band[slot:], preferred_element_type=jnp.float32)
        ).astype(jnp.bfloat16)
        pred_low = row_pass(rowf_ref, low, rank_count, slot)
        pred_high = row_pass(rowf_ref, high, rank_count, slot)
        pred_own = pltpu.roll(jnp.where(lane < HALF, pred_high, pred_low), HALF, 1)
        res_own = (dirty_ref[c].astype(jnp.float32) - pred_own).astype(jnp.bfloat16)
        res_ref[c] = res_own
        dl = unpack_cols(left_ref[c, rows:]).astype(jnp.float32)
        dr = unpack_cols(right_ref[c, rows:]).astype(jnp.float32)
        halo_l = jnp.where(sky_index > 0, dl - pred_low[:, :HALF], 0.0)
        pred_right = pltpu.roll(pred_high, slot - HALF, 1)[:, :HALF]
        halo_r = jnp.where(sky_index < sky_count - 1, dr - pred_right, 0.0)
        adj = cola_ref[...]
        col_pass = (
            jnp.dot(halo_l.astype(jnp.bfloat16), adj[:HALF], preferred_element_type=jnp.float32)
            + jnp.dot(res_own, adj[HALF : HALF + slot], preferred_element_type=jnp.float32)
            + jnp.dot(halo_r.astype(jnp.bfloat16), adj[HALF + slot :], preferred_element_type=jnp.float32)
        ).astype(jnp.bfloat16)
        grad_chan = row_pass(rowa_ref, col_pass, rank_count, slot)
        for j in range(pieces):
            block = grad_chan[j * piece_rows : (j + 1) * piece_rows]
            for b in range(basis):
                term = spec_ref[first_chan + c, b] * block
                if c == 0:
                    part_ref[j, b] = term
                else:
                    part_ref[j, b] = part_ref[j, b] + term


def vmem_spec():
    return pl.BlockSpec(memory_space=pltpu.VMEM)


def smem_spec():
    return pl.BlockSpec(memory_space=pltpu.SMEM)


def body(dirty, model, spectral, psf_rows, psf_cols, strip_width):
    local_chans, row_count, slot_width = dirty.shape
    basis = model.shape[0]
    rank_count = psf_rows.shape[1]
    chan_count = lax.axis_size("chan")
    sky_count = lax.axis_size("sky")

    image_rows = spectral[:, 0][:, None, None] * model[0][None]
    for basis_idx in range(1, basis):
        image_rows = image_rows + spectral[:, basis_idx][:, None, None] * model[basis_idx][None]
    image_rows = image_rows.astype(jnp.bfloat16)
    image = lax.all_to_all(image_rows, "chan", 0, 1, tiled=True)
    def with_dirty(cols):
        return jnp.concatenate([image, jnp.concatenate([cols[:, : row_count // 2], cols[:, row_count // 2 :]], axis=2)], axis=1)

    to_right = with_dirty(dirty[:, :, slot_width - HALF :])
    to_left = with_dirty(dirty[:, :, :HALF])
    left = from_behind(to_right, "sky", 1)
    right = from_behind(to_left, "sky", -1)

    taps = jnp.concatenate([psf_rows, psf_cols], axis=1)
    taps = jnp.pad(taps, ((0, 0), (0, 0), (0, LANES - TAPS)))
    piece_rows = row_count // chan_count
    ext = slot_width + 2 * HALF
    residual, partial_value = pl.pallas_call(
        functools.partial(main_kernel, rank_count, local_chans, sky_count),
        out_shape=(
            jax.ShapeDtypeStruct(dirty.shape, jnp.bfloat16),
            jax.ShapeDtypeStruct((chan_count, basis, piece_rows, slot_width), jnp.float32),
        ),
        in_specs=[smem_spec()] + [vmem_spec()] * 5,
        out_specs=[vmem_spec()] * 2,
        scratch_shapes=[
            pltpu.VMEM((ext, rank_count * slot_width), jnp.bfloat16),
            pltpu.VMEM((rank_count, row_count, row_count), jnp.bfloat16),
            pltpu.VMEM((ext, rank_count * slot_width), jnp.bfloat16),
            pltpu.VMEM((rank_count, row_count, row_count), jnp.bfloat16),
        ],
    )(spectral, taps, left, image, right, dirty)

    pieces = lax.all_to_all(partial_value, "chan", 0, 0, tiled=True)
    grad_share = pieces.sum(0)

    gram_rows = jnp.einsum("crt,cst->crs", psf_rows, psf_rows, precision=lax.Precision.HIGHEST)
    gram_cols = jnp.einsum("crt,cst->crs", psf_cols, psf_cols, precision=lax.Precision.HIGHEST)
    energy = jnp.sum(gram_rows * gram_cols, axis=(1, 2))
    curvature = jnp.sum(spectral * spectral * energy[:, None], axis=0)
    model_new = model + grad_share / curvature[:, None, None]
    return (residual, model_new)


def solution(mesh):
    placed = (P("chan", None, "sky"), P(None, "chan", "sky"), P(), P(), P(), P())
    return jax.shard_map(
        body,
        mesh=mesh,
        in_specs=placed,
        out_specs=(P("chan", None, "sky"), P(None, "chan", "sky")),
        check_vma=False,
    )
```

```python
import functools

import jax
import jax.numpy as jnp
from jax import lax
from jax.experimental import pallas as pl
from jax.experimental.pallas import tpu as pltpu
from jax.sharding import PartitionSpec as P

TAPS = 129
HALF = (TAPS - 1) // 2
LANES = 512


def from_behind(value, axis, steps):
    count = lax.axis_size(axis)
    first, last = (max(0, -steps), min(count, count - steps))
    return lax.ppermute(value, axis, [(source, source + steps) for source in range(first, last)])


def col_band(w, slot):
    ext = slot + 2 * HALF
    spread = jnp.broadcast_to(w[:, :ext], (ext, ext))
    return pltpu.roll(spread, ext - 2 * HALF, 1, stride=1, stride_axis=0)[:, :slot]


def row_band(w, rows):
    spread = jnp.broadcast_to(w, (rows, LANES))
    return pltpu.roll(spread, LANES - HALF, 1, stride=1, stride_axis=0)[:, :rows]


def row_pass(row_ref, col_pass, rank_count, slot):
    total = None
    for r in range(rank_count):
        part = jnp.dot(
            row_ref[r], col_pass[:, r * slot : (r + 1) * slot], preferred_element_type=jnp.float32
        )
        total = part if total is None else total + part
    return total


def unpack_cols(packed):
    return jnp.concatenate([packed[:, :HALF], pltpu.roll(packed, HALF, 1)[:, :HALF]], axis=0)


def band_kernel(rank_count, local_chans, slot, taps_ref, colf_ref, rowf_ref, cola_ref, rowa_ref):
    rows = rowf_ref.shape[-1]
    first_chan = lax.axis_index("chan") * local_chans
    flip = (
        lax.broadcasted_iota(jnp.int32, (LANES // 2, LANES), 0)
        + lax.broadcasted_iota(jnp.int32, (LANES // 2, LANES), 1)
        == TAPS - 1
    ).astype(jnp.bfloat16)
    for c in range(local_chans):
        taps = taps_ref[first_chan + c].astype(jnp.bfloat16)
        rev = jnp.dot(taps[:, : LANES // 2], flip, preferred_element_type=jnp.float32)
        taps = taps.astype(jnp.float32)
        for r in range(rank_count):
            u, v = taps[r : r + 1], taps[rank_count + r : rank_count + r + 1]
            u_rev, v_rev = rev[r : r + 1], rev[rank_count + r : rank_count + r + 1]
            colf_ref[c, :, r * slot : (r + 1) * slot] = col_band(v_rev, slot).astype(jnp.bfloat16)
            cola_ref[c, :, r * slot : (r + 1) * slot] = col_band(v, slot).astype(jnp.bfloat16)
            rowf_ref[c, r] = row_band(u, rows).astype(jnp.bfloat16)
            rowa_ref[c, r] = row_band(u_rev, rows).astype(jnp.bfloat16)


def main_kernel(
    rank_count, local_chans, sky_count, spec_ref, colf_ref, rowf_ref, cola_ref, rowa_ref,
    left_ref, xc_ref, right_ref, dirty_ref, res_ref, part_ref,
):
    slot = xc_ref.shape[-1]
    rows = xc_ref.shape[1]
    pieces, basis, piece_rows, _ = part_ref.shape
    first_chan = lax.axis_index("chan") * local_chans
    sky_index = lax.axis_index("sky")
    lane = lax.broadcasted_iota(jnp.int32, (rows, slot), 1)
    for c in range(local_chans):
        band = colf_ref[c]
        xl, xc, xr = left_ref[c, :rows], xc_ref[c], right_ref[c, :rows]
        low = (
            jnp.dot(xl, band[:slot], preferred_element_type=jnp.float32)
            + jnp.dot(xc, band[slot:], preferred_element_type=jnp.float32)
        ).astype(jnp.bfloat16)
        high = (
            jnp.dot(xc, band[:slot], preferred_element_type=jnp.float32)
            + jnp.dot(xr, band[slot:], preferred_element_type=jnp.float32)
        ).astype(jnp.bfloat16)
        pred_low = row_pass(rowf_ref.at[c], low, rank_count, slot)
        pred_high = row_pass(rowf_ref.at[c], high, rank_count, slot)
        pred_own = pltpu.roll(jnp.where(lane < HALF, pred_high, pred_low), HALF, 1)
        res_own = (dirty_ref[c].astype(jnp.float32) - pred_own).astype(jnp.bfloat16)
        res_ref[c] = res_own
        dl = unpack_cols(left_ref[c, rows:]).astype(jnp.float32)
        dr = unpack_cols(right_ref[c, rows:]).astype(jnp.float32)
        halo_l = jnp.where(sky_index > 0, dl - pred_low[:, :HALF], 0.0)
        pred_right = pltpu.roll(pred_high, slot - HALF, 1)[:, :HALF]
        halo_r = jnp.where(sky_index < sky_count - 1, dr - pred_right, 0.0)
        adj = cola_ref[c]
        col_pass = (
            jnp.dot(halo_l.astype(jnp.bfloat16), adj[:HALF], preferred_element_type=jnp.float32)
            + jnp.dot(res_own, adj[HALF : HALF + slot], preferred_element_type=jnp.float32)
            + jnp.dot(halo_r.astype(jnp.bfloat16), adj[HALF + slot :], preferred_element_type=jnp.float32)
        ).astype(jnp.bfloat16)
        grad_chan = row_pass(rowa_ref.at[c], col_pass, rank_count, slot)
        for j in range(pieces):
            block = grad_chan[j * piece_rows : (j + 1) * piece_rows]
            for b in range(basis):
                term = spec_ref[first_chan + c, b] * block
                if c == 0:
                    part_ref[j, b] = term
                else:
                    part_ref[j, b] = part_ref[j, b] + term


def vmem_spec():
    return pl.BlockSpec(memory_space=pltpu.VMEM)


def smem_spec():
    return pl.BlockSpec(memory_space=pltpu.SMEM)


def body(dirty, model, spectral, psf_rows, psf_cols, strip_width):
    local_chans, row_count, slot_width = dirty.shape
    basis = model.shape[0]
    rank_count = psf_rows.shape[1]
    chan_count = lax.axis_size("chan")
    sky_count = lax.axis_size("sky")

    image_rows = spectral[:, 0][:, None, None] * model[0][None]
    for basis_idx in range(1, basis):
        image_rows = image_rows + spectral[:, basis_idx][:, None, None] * model[basis_idx][None]
    image_rows = image_rows.astype(jnp.bfloat16)
    image = lax.all_to_all(image_rows, "chan", 0, 1, tiled=True)
    def with_dirty(cols):
        return jnp.concatenate([image, jnp.concatenate([cols[:, : row_count // 2], cols[:, row_count // 2 :]], axis=2)], axis=1)

    to_right = with_dirty(dirty[:, :, slot_width - HALF :])
    to_left = with_dirty(dirty[:, :, :HALF])
    left = from_behind(to_right, "sky", 1)
    right = from_behind(to_left, "sky", -1)

    taps = jnp.concatenate([psf_rows, psf_cols], axis=1)
    taps = jnp.pad(taps, ((0, 0), (0, 0), (0, LANES - TAPS)))
    piece_rows = row_count // chan_count
    ext = slot_width + 2 * HALF
    band_shapes = (
        jax.ShapeDtypeStruct((local_chans, ext, rank_count * slot_width), jnp.bfloat16),
        jax.ShapeDtypeStruct((local_chans, rank_count, row_count, row_count), jnp.bfloat16),
    )
    bands = pl.pallas_call(
        functools.partial(band_kernel, rank_count, local_chans, slot_width),
        out_shape=band_shapes * 2,
        in_specs=[vmem_spec()],
        out_specs=[vmem_spec()] * 4,
    )(taps)
    residual, partial_value = pl.pallas_call(
        functools.partial(main_kernel, rank_count, local_chans, sky_count),
        out_shape=(
            jax.ShapeDtypeStruct(dirty.shape, jnp.bfloat16),
            jax.ShapeDtypeStruct((chan_count, basis, piece_rows, slot_width), jnp.float32),
        ),
        in_specs=[smem_spec()] + [vmem_spec()] * 8,
        out_specs=[vmem_spec()] * 2,
    )(spectral, *bands, left, image, right, dirty)

    pieces = lax.all_to_all(partial_value, "chan", 0, 0, tiled=True)
    grad_share = pieces.sum(0)

    gram_rows = jnp.einsum("crt,cst->crs", psf_rows, psf_rows, precision=lax.Precision.HIGHEST)
    gram_cols = jnp.einsum("crt,cst->crs", psf_cols, psf_cols, precision=lax.Precision.HIGHEST)
    energy = jnp.sum(gram_rows * gram_cols, axis=(1, 2))
    curvature = jnp.sum(spectral * spectral * energy[:, None], axis=0)
    model_new = model + grad_share / curvature[:, None, None]
    return (residual, model_new)


def solution(mesh):
    placed = (P("chan", None, "sky"), P(None, "chan", "sky"), P(), P(), P(), P())
    return jax.shard_map(
        body,
        mesh=mesh,
        in_specs=placed,
        out_specs=(P("chan", None, "sky"), P(None, "chan", "sky")),
        check_vma=False,
    )
```

```python
import functools

import jax
import jax.numpy as jnp
from jax import lax
from jax.experimental import pallas as pl
from jax.experimental.pallas import tpu as pltpu
from jax.sharding import PartitionSpec as P

TAPS = 129
HALF = (TAPS - 1) // 2
LANES = 512


def from_behind(value, axis, steps):
    count = lax.axis_size(axis)
    first, last = (max(0, -steps), min(count, count - steps))
    return lax.ppermute(value, axis, [(source, source + steps) for source in range(first, last)])


def col_band(w, slot):
    ext = slot + 2 * HALF
    spread = jnp.broadcast_to(w[:, :ext], (ext, ext))
    return pltpu.roll(spread, ext - 2 * HALF, 1, stride=1, stride_axis=0)[:, :slot]


def row_band(w, rows):
    spread = jnp.broadcast_to(w, (rows, LANES))
    return pltpu.roll(spread, LANES - HALF, 1, stride=1, stride_axis=0)[:, :rows]


def row_pass(row_ref, col_pass, rank_count, slot):
    total = None
    for r in range(rank_count):
        part = jnp.dot(
            row_ref[r], col_pass[:, r * slot : (r + 1) * slot], preferred_element_type=jnp.float32
        )
        total = part if total is None else total + part
    return total


def band_kernel(rank_count, local_chans, slot, taps_ref, colf_ref, rowf_ref, cola_ref, rowa_ref):
    rows = rowf_ref.shape[-1]
    first_chan = lax.axis_index("chan") * local_chans
    flip = (
        lax.broadcasted_iota(jnp.int32, (LANES // 2, LANES), 0)
        + lax.broadcasted_iota(jnp.int32, (LANES // 2, LANES), 1)
        == TAPS - 1
    ).astype(jnp.bfloat16)
    for c in range(local_chans):
        taps = taps_ref[first_chan + c].astype(jnp.bfloat16)
        rev = jnp.dot(taps[:, : LANES // 2], flip, preferred_element_type=jnp.float32)
        taps = taps.astype(jnp.float32)
        for r in range(rank_count):
            u, v = taps[r : r + 1], taps[rank_count + r : rank_count + r + 1]
            u_rev, v_rev = rev[r : r + 1], rev[rank_count + r : rank_count + r + 1]
            colf_ref[c, :, r * slot : (r + 1) * slot] = col_band(v_rev, slot).astype(jnp.bfloat16)
            cola_ref[c, :, r * slot : (r + 1) * slot] = col_band(v, slot).astype(jnp.bfloat16)
            rowf_ref[c, r] = row_band(u, rows).astype(jnp.bfloat16)
            rowa_ref[c, r] = row_band(u_rev, rows).astype(jnp.bfloat16)


def main_kernel(
    rank_count, local_chans, sky_count, spec_ref, colf_ref, rowf_ref, cola_ref, rowa_ref,
    left_ref, xc_ref, right_ref, dirty_ref, res_ref, part_ref,
):
    slot = xc_ref.shape[-1]
    rows = xc_ref.shape[1]
    pieces, basis, piece_rows, _ = part_ref.shape
    first_chan = lax.axis_index("chan") * local_chans
    sky_index = lax.axis_index("sky")
    lane = lax.broadcasted_iota(jnp.int32, (rows, slot), 1)
    for c in range(local_chans):
        xl, xc, xr = left_ref[c, :rows], xc_ref[c], right_ref[c, :rows]
        stacked = jnp.concatenate(
            [jnp.concatenate([xl, xc], axis=1), jnp.concatenate([xc, xr], axis=1)], axis=0
        )
        col_pass = jnp.dot(stacked, colf_ref[c], preferred_element_type=jnp.float32).astype(jnp.bfloat16)
        pred = None
        for r in range(rank_count):
            both = jnp.concatenate(
                [col_pass[:rows, r * slot : (r + 1) * slot], col_pass[rows:, r * slot : (r + 1) * slot]], axis=1
            )
            part = jnp.dot(rowf_ref[c, r], both, preferred_element_type=jnp.float32)
            pred = part if pred is None else pred + part
        pred_low, pred_high = pred[:, :slot], pred[:, slot:]
        pred_own = pltpu.roll(jnp.where(lane < HALF, pred_high, pred_low), HALF, 1)
        res_own = (dirty_ref[c].astype(jnp.float32) - pred_own).astype(jnp.bfloat16)
        res_ref[c] = res_own
        packed_l, packed_r = left_ref[c, rows:], right_ref[c, rows:]
        dl = jnp.concatenate([packed_l, pltpu.roll(packed_l, HALF, 1)], axis=0).astype(jnp.float32)
        dr = jnp.concatenate([pltpu.roll(packed_r, HALF, 1), packed_r], axis=0).astype(jnp.float32)
        halo_l = jnp.where(sky_index > 0, dl - pred_low, 0.0).astype(jnp.bfloat16)
        halo_r = jnp.where(sky_index < sky_count - 1, dr - pred_high, 0.0).astype(jnp.bfloat16)
        shifted = pltpu.roll(res_own, HALF, 1)
        res_low = jnp.where(lane < HALF, halo_l, shifted)
        res_high = jnp.where(lane < HALF, shifted, halo_r)
        adj_in = jnp.concatenate([res_low, res_high], axis=1)
        adj_pass = jnp.dot(adj_in, cola_ref[c], preferred_element_type=jnp.float32).astype(jnp.bfloat16)
        grad_chan = row_pass(rowa_ref.at[c], adj_pass, rank_count, slot)
        for j in range(pieces):
            block = grad_chan[j * piece_rows : (j + 1) * piece_rows]
            for b in range(basis):
                term = spec_ref[first_chan + c, b] * block
                if c == 0:
                    part_ref[j, b] = term
                else:
                    part_ref[j, b] = part_ref[j, b] + term


def vmem_spec():
    return pl.BlockSpec(memory_space=pltpu.VMEM)


def smem_spec():
    return pl.BlockSpec(memory_space=pltpu.SMEM)


def body(dirty, model, spectral, psf_rows, psf_cols, strip_width):
    local_chans, row_count, slot_width = dirty.shape
    basis = model.shape[0]
    rank_count = psf_rows.shape[1]
    chan_count = lax.axis_size("chan")
    sky_count = lax.axis_size("sky")

    image_rows = spectral[:, 0][:, None, None] * model[0][None]
    for basis_idx in range(1, basis):
        image_rows = image_rows + spectral[:, basis_idx][:, None, None] * model[basis_idx][None]
    image_rows = image_rows.astype(jnp.bfloat16)
    image = lax.all_to_all(image_rows, "chan", 0, 1, tiled=True)
    def with_dirty(cols):
        return jnp.concatenate([image, jnp.concatenate([cols[:, : row_count // 2], cols[:, row_count // 2 :]], axis=2)], axis=1)

    to_right = with_dirty(dirty[:, :, slot_width - HALF :])
    to_left = with_dirty(dirty[:, :, :HALF])
    left = from_behind(to_right, "sky", 1)
    right = from_behind(to_left, "sky", -1)

    taps = jnp.concatenate([psf_rows, psf_cols], axis=1)
    taps = jnp.pad(taps, ((0, 0), (0, 0), (0, LANES - TAPS)))
    piece_rows = row_count // chan_count
    ext = slot_width + 2 * HALF
    band_shapes = (
        jax.ShapeDtypeStruct((local_chans, ext, rank_count * slot_width), jnp.bfloat16),
        jax.ShapeDtypeStruct((local_chans, rank_count, row_count, row_count), jnp.bfloat16),
    )
    bands = pl.pallas_call(
        functools.partial(band_kernel, rank_count, local_chans, slot_width),
        out_shape=band_shapes * 2,
        in_specs=[vmem_spec()],
        out_specs=[vmem_spec()] * 4,
    )(taps)
    residual, partial_value = pl.pallas_call(
        functools.partial(main_kernel, rank_count, local_chans, sky_count),
        out_shape=(
            jax.ShapeDtypeStruct(dirty.shape, jnp.bfloat16),
            jax.ShapeDtypeStruct((chan_count, basis, piece_rows, slot_width), jnp.float32),
        ),
        in_specs=[smem_spec()] + [vmem_spec()] * 8,
        out_specs=[vmem_spec()] * 2,
    )(spectral, *bands, left, image, right, dirty)

    pieces = lax.all_to_all(partial_value, "chan", 0, 0, tiled=True)
    grad_share = pieces.sum(0)

    gram_rows = jnp.einsum("crt,cst->crs", psf_rows, psf_rows, precision=lax.Precision.HIGHEST)
    gram_cols = jnp.einsum("crt,cst->crs", psf_cols, psf_cols, precision=lax.Precision.HIGHEST)
    energy = jnp.sum(gram_rows * gram_cols, axis=(1, 2))
    curvature = jnp.sum(spectral * spectral * energy[:, None], axis=0)
    model_new = model + grad_share / curvature[:, None, None]
    return (residual, model_new)


def solution(mesh):
    placed = (P("chan", None, "sky"), P(None, "chan", "sky"), P(), P(), P(), P())
    return jax.shard_map(
        body,
        mesh=mesh,
        in_specs=placed,
        out_specs=(P("chan", None, "sky"), P(None, "chan", "sky")),
        check_vma=False,
    )
```

```python
import functools

import jax
import jax.numpy as jnp
from jax import lax
from jax.experimental import pallas as pl
from jax.experimental.pallas import tpu as pltpu
from jax.sharding import PartitionSpec as P

TAPS = 129
HALF = (TAPS - 1) // 2
LANES = 512


def from_behind(value, axis, steps):
    count = lax.axis_size(axis)
    first, last = (max(0, -steps), min(count, count - steps))
    return lax.ppermute(value, axis, [(source, source + steps) for source in range(first, last)])


def col_band(w, slot):
    ext = slot + 2 * HALF
    spread = jnp.broadcast_to(w[:, :ext], (ext, ext))
    return pltpu.roll(spread, ext - 2 * HALF, 1, stride=1, stride_axis=0)[:, :slot]


def row_band(w, rows):
    spread = jnp.broadcast_to(w, (rows, LANES))
    return pltpu.roll(spread, LANES - HALF, 1, stride=1, stride_axis=0)[:, :rows]


def row_pass(row_ref, col_pass, rank_count, slot):
    total = None
    for r in range(rank_count):
        part = jnp.dot(
            row_ref[r], col_pass[:, r * slot : (r + 1) * slot], preferred_element_type=jnp.float32
        )
        total = part if total is None else total + part
    return total


def band_kernel(rank_count, local_chans, slot, taps_ref, colf_ref, rowf_ref, cola_ref, rowa_ref):
    rows = rowf_ref.shape[-1]
    first_chan = lax.axis_index("chan") * local_chans
    flip = (
        lax.broadcasted_iota(jnp.int32, (LANES // 2, LANES), 0)
        + lax.broadcasted_iota(jnp.int32, (LANES // 2, LANES), 1)
        == TAPS - 1
    ).astype(jnp.bfloat16)
    for c in range(local_chans):
        taps = taps_ref[first_chan + c].astype(jnp.bfloat16)
        rev = jnp.dot(taps[:, : LANES // 2], flip, preferred_element_type=jnp.float32)
        taps = taps.astype(jnp.float32)
        for r in range(rank_count):
            u, v = taps[r : r + 1], taps[rank_count + r : rank_count + r + 1]
            u_rev, v_rev = rev[r : r + 1], rev[rank_count + r : rank_count + r + 1]
            colf_ref[c, :, r * slot : (r + 1) * slot] = col_band(v_rev, slot).astype(jnp.bfloat16)
            cola_ref[c, :, r * slot : (r + 1) * slot] = col_band(v, slot).astype(jnp.bfloat16)
            rowf_ref[c, r] = row_band(u, rows).astype(jnp.bfloat16)
            rowa_ref[c, r] = row_band(u_rev, rows).astype(jnp.bfloat16)


def main_kernel(
    rank_count, local_chans, sky_count, spec_ref, colf_ref, rowf_ref, cola_ref, rowa_ref,
    left_ref, xc_ref, right_ref, dirty_ref, res_ref, part_ref,
):
    slot = xc_ref.shape[-1]
    rows = xc_ref.shape[0]
    pieces, basis, piece_rows, _ = part_ref.shape
    first_chan = lax.axis_index("chan") * local_chans
    sky_index = lax.axis_index("sky")
    lane = lax.broadcasted_iota(jnp.int32, (rows, slot), 1)
    step = pl.program_id(0)
    if True:
        xl, xc, xr = left_ref[:rows], xc_ref[...], right_ref[:rows]
        stacked = jnp.concatenate(
            [jnp.concatenate([xl, xc], axis=1), jnp.concatenate([xc, xr], axis=1)], axis=0
        )
        col_pass = jnp.dot(stacked, colf_ref[...], preferred_element_type=jnp.float32).astype(jnp.bfloat16)
        pred = None
        for r in range(rank_count):
            both = jnp.concatenate(
                [col_pass[:rows, r * slot : (r + 1) * slot], col_pass[rows:, r * slot : (r + 1) * slot]], axis=1
            )
            part = jnp.dot(rowf_ref[r], both, preferred_element_type=jnp.float32)
            pred = part if pred is None else pred + part
        pred_low, pred_high = pred[:, :slot], pred[:, slot:]
        pred_own = pltpu.roll(jnp.where(lane < HALF, pred_high, pred_low), HALF, 1)
        res_own = (dirty_ref[...].astype(jnp.float32) - pred_own).astype(jnp.bfloat16)
        res_ref[...] = res_own
        packed_l, packed_r = left_ref[rows:], right_ref[rows:]
        dl = jnp.concatenate([packed_l, pltpu.roll(packed_l, HALF, 1)], axis=0).astype(jnp.float32)
        dr = jnp.concatenate([pltpu.roll(packed_r, HALF, 1), packed_r], axis=0).astype(jnp.float32)
        halo_l = jnp.where(sky_index > 0, dl - pred_low, 0.0).astype(jnp.bfloat16)
        halo_r = jnp.where(sky_index < sky_count - 1, dr - pred_high, 0.0).astype(jnp.bfloat16)
        shifted = pltpu.roll(res_own, HALF, 1)
        res_low = jnp.where(lane < HALF, halo_l, shifted)
        res_high = jnp.where(lane < HALF, shifted, halo_r)
        adj_in = jnp.concatenate([res_low, res_high], axis=1)
        adj_pass = jnp.dot(adj_in, cola_ref[...], preferred_element_type=jnp.float32).astype(jnp.bfloat16)
        grad_chan = row_pass(rowa_ref, adj_pass, rank_count, slot)
        @pl.when(step == 0)
        def _():
            for j in range(pieces):
                block = grad_chan[j * piece_rows : (j + 1) * piece_rows]
                for b in range(basis):
                    part_ref[j, b] = spec_ref[first_chan, b] * block

        @pl.when(step > 0)
        def _():
            for j in range(pieces):
                block = grad_chan[j * piece_rows : (j + 1) * piece_rows]
                for b in range(basis):
                    part_ref[j, b] = part_ref[j, b] + spec_ref[first_chan + step, b] * block


def vmem_spec():
    return pl.BlockSpec(memory_space=pltpu.VMEM)


def per_chan(shape):
    return pl.BlockSpec((None,) + tuple(shape[1:]), lambda c: (c,) + (0,) * (len(shape) - 1))


def smem_spec():
    return pl.BlockSpec(memory_space=pltpu.SMEM)


def body(dirty, model, spectral, psf_rows, psf_cols, strip_width):
    local_chans, row_count, slot_width = dirty.shape
    basis = model.shape[0]
    rank_count = psf_rows.shape[1]
    chan_count = lax.axis_size("chan")
    sky_count = lax.axis_size("sky")

    image_rows = spectral[:, 0][:, None, None] * model[0][None]
    for basis_idx in range(1, basis):
        image_rows = image_rows + spectral[:, basis_idx][:, None, None] * model[basis_idx][None]
    image_rows = image_rows.astype(jnp.bfloat16)
    image = lax.all_to_all(image_rows, "chan", 0, 1, tiled=True)
    def with_dirty(cols):
        return jnp.concatenate([image, jnp.concatenate([cols[:, : row_count // 2], cols[:, row_count // 2 :]], axis=2)], axis=1)

    to_right = with_dirty(dirty[:, :, slot_width - HALF :])
    to_left = with_dirty(dirty[:, :, :HALF])
    left = from_behind(to_right, "sky", 1)
    right = from_behind(to_left, "sky", -1)

    taps = jnp.concatenate([psf_rows, psf_cols], axis=1)
    taps = jnp.pad(taps, ((0, 0), (0, 0), (0, LANES - TAPS)))
    piece_rows = row_count // chan_count
    ext = slot_width + 2 * HALF
    band_shapes = (
        jax.ShapeDtypeStruct((local_chans, ext, rank_count * slot_width), jnp.bfloat16),
        jax.ShapeDtypeStruct((local_chans, rank_count, row_count, row_count), jnp.bfloat16),
    )
    bands = pl.pallas_call(
        functools.partial(band_kernel, rank_count, local_chans, slot_width),
        out_shape=band_shapes * 2,
        in_specs=[vmem_spec()],
        out_specs=[vmem_spec()] * 4,
    )(taps)
    residual, partial_value = pl.pallas_call(
        functools.partial(main_kernel, rank_count, local_chans, sky_count),
        out_shape=(
            jax.ShapeDtypeStruct(dirty.shape, jnp.bfloat16),
            jax.ShapeDtypeStruct((chan_count, basis, piece_rows, slot_width), jnp.float32),
        ),
        grid=(local_chans,),
        in_specs=[smem_spec()] + [per_chan(a.shape) for a in (*bands, left, image, right, dirty)],
        out_specs=[
            per_chan(dirty.shape),
            pl.BlockSpec((chan_count, basis, piece_rows, slot_width), lambda c: (0, 0, 0, 0)),
        ],
    )(spectral, *bands, left, image, right, dirty)

    pieces = lax.all_to_all(partial_value, "chan", 0, 0, tiled=True)
    grad_share = pieces.sum(0)

    gram_rows = jnp.einsum("crt,cst->crs", psf_rows, psf_rows, precision=lax.Precision.HIGHEST)
    gram_cols = jnp.einsum("crt,cst->crs", psf_cols, psf_cols, precision=lax.Precision.HIGHEST)
    energy = jnp.sum(gram_rows * gram_cols, axis=(1, 2))
    curvature = jnp.sum(spectral * spectral * energy[:, None], axis=0)
    model_new = model + grad_share / curvature[:, None, None]
    return (residual, model_new)


def solution(mesh):
    placed = (P("chan", None, "sky"), P(None, "chan", "sky"), P(), P(), P(), P())
    return jax.shard_map(
        body,
        mesh=mesh,
        in_specs=placed,
        out_specs=(P("chan", None, "sky"), P(None, "chan", "sky")),
        check_vma=False,
    )
```

```python
import functools

import jax
import jax.numpy as jnp
from jax import lax
from jax.experimental import pallas as pl
from jax.experimental.pallas import tpu as pltpu
from jax.sharding import PartitionSpec as P

TAPS = 129
HALF = (TAPS - 1) // 2
LANES = 512


def from_behind(value, axis, steps):
    count = lax.axis_size(axis)
    first, last = (max(0, -steps), min(count, count - steps))
    return lax.ppermute(value, axis, [(source, source + steps) for source in range(first, last)])


def col_band(w, slot):
    ext = slot + 2 * HALF
    spread = jnp.broadcast_to(w[:, :ext], (ext, ext))
    return pltpu.roll(spread, ext - 2 * HALF, 1, stride=1, stride_axis=0)[:, :slot]


def row_band(w, rows):
    spread = jnp.broadcast_to(w, (rows, LANES))
    return pltpu.roll(spread, LANES - HALF, 1, stride=1, stride_axis=0)[:, :rows]


def row_pass(row_ref, col_pass, rank_count, slot):
    total = None
    for r in range(rank_count):
        part = jnp.dot(
            row_ref[r], col_pass[:, r * slot : (r + 1) * slot], preferred_element_type=jnp.float32
        )
        total = part if total is None else total + part
    return total


def band_kernel(rank_count, local_chans, slot, taps_ref, colf_ref, rowf_ref, cola_ref, rowa_ref):
    rows = rowf_ref.shape[-1]
    first_chan = lax.axis_index("chan") * local_chans
    flip = (
        lax.broadcasted_iota(jnp.int32, (LANES // 2, LANES), 0)
        + lax.broadcasted_iota(jnp.int32, (LANES // 2, LANES), 1)
        == TAPS - 1
    ).astype(jnp.bfloat16)
    for c in range(local_chans):
        taps = taps_ref[first_chan + c].astype(jnp.bfloat16)
        rev = jnp.dot(taps[:, : LANES // 2], flip, preferred_element_type=jnp.float32)
        taps = taps.astype(jnp.float32)
        for r in range(rank_count):
            u, v = taps[r : r + 1], taps[rank_count + r : rank_count + r + 1]
            u_rev, v_rev = rev[r : r + 1], rev[rank_count + r : rank_count + r + 1]
            colf_ref[c, :, r * slot : (r + 1) * slot] = col_band(v_rev, slot).astype(jnp.bfloat16)
            cola_ref[c, :, r * slot : (r + 1) * slot] = col_band(v, slot).astype(jnp.bfloat16)
            rowf_ref[c, r] = row_band(u, rows).astype(jnp.bfloat16)
            rowa_ref[c, r] = row_band(u_rev, rows).astype(jnp.bfloat16)


def main_kernel(
    rank_count, local_chans, sky_count, spec_ref, colf_ref, rowf_ref, cola_ref, rowa_ref,
    left_ref, xc_ref, right_ref, dirty_ref, res_ref, part_ref,
):
    slot = xc_ref.shape[-1]
    rows = xc_ref.shape[0]
    pieces, basis, piece_rows, _ = part_ref.shape
    first_chan = lax.axis_index("chan") * local_chans
    sky_index = lax.axis_index("sky")
    lane = lax.broadcasted_iota(jnp.int32, (rows, slot), 1)
    step = pl.program_id(0)
    if True:
        xl, xc, xr = left_ref[:rows], xc_ref[...], right_ref[:rows]
        stacked = jnp.concatenate(
            [jnp.concatenate([xl, xc], axis=1), jnp.concatenate([xc, xr], axis=1)], axis=0
        )
        col_pass = jnp.dot(stacked, colf_ref[...], preferred_element_type=jnp.float32).astype(jnp.bfloat16)
        pred = None
        for r in range(rank_count):
            both = jnp.concatenate(
                [col_pass[:rows, r * slot : (r + 1) * slot], col_pass[rows:, r * slot : (r + 1) * slot]], axis=1
            )
            part = jnp.dot(rowf_ref[r], both, preferred_element_type=jnp.float32)
            pred = part if pred is None else pred + part
        pred_low, pred_high = pred[:, :slot], pred[:, slot:]
        pred_own = pltpu.roll(jnp.where(lane < HALF, pred_high, pred_low), HALF, 1)
        res_own = (dirty_ref[...].astype(jnp.float32) - pred_own).astype(jnp.bfloat16)
        res_ref[...] = res_own
        packed_l, packed_r = left_ref[rows:], right_ref[rows:]
        dl = jnp.concatenate([packed_l, pltpu.roll(packed_l, HALF, 1)], axis=0).astype(jnp.float32)
        dr = jnp.concatenate([pltpu.roll(packed_r, HALF, 1), packed_r], axis=0).astype(jnp.float32)
        halo_l = jnp.where(sky_index > 0, dl - pred_low, 0.0).astype(jnp.bfloat16)
        halo_r = jnp.where(sky_index < sky_count - 1, dr - pred_high, 0.0).astype(jnp.bfloat16)
        shifted = pltpu.roll(res_own, HALF, 1)
        res_low = jnp.where(lane < HALF, halo_l, shifted)
        res_high = jnp.where(lane < HALF, shifted, halo_r)
        adj_in = jnp.concatenate([res_low, res_high], axis=1)
        adj_pass = jnp.dot(adj_in, cola_ref[...], preferred_element_type=jnp.float32).astype(jnp.bfloat16)
        grad_chan = row_pass(rowa_ref, adj_pass, rank_count, slot)
        @pl.when(step == 0)
        def _():
            for j in range(pieces):
                block = grad_chan[j * piece_rows : (j + 1) * piece_rows]
                for b in range(basis):
                    part_ref[j, b] = spec_ref[first_chan, b] * block

        @pl.when(step > 0)
        def _():
            for j in range(pieces):
                block = grad_chan[j * piece_rows : (j + 1) * piece_rows]
                for b in range(basis):
                    part_ref[j, b] = part_ref[j, b] + spec_ref[first_chan + step, b] * block


def vmem_spec():
    return pl.BlockSpec(memory_space=pltpu.VMEM)


def update_kernel(curv_ref, pieces_ref, model_ref, out_ref):
    for b in range(out_ref.shape[0]):
        grad = pieces_ref[0, b]
        for j in range(1, pieces_ref.shape[0]):
            grad = grad + pieces_ref[j, b]
        out_ref[b] = model_ref[b] + grad / curv_ref[b]


def per_chan(shape):
    return pl.BlockSpec((None,) + tuple(shape[1:]), lambda c: (c,) + (0,) * (len(shape) - 1))


def smem_spec():
    return pl.BlockSpec(memory_space=pltpu.SMEM)


def body(dirty, model, spectral, psf_rows, psf_cols, strip_width):
    local_chans, row_count, slot_width = dirty.shape
    basis = model.shape[0]
    rank_count = psf_rows.shape[1]
    chan_count = lax.axis_size("chan")
    sky_count = lax.axis_size("sky")

    model_full = lax.all_gather(model, "chan", axis=1, tiled=True)
    spec_local = lax.dynamic_slice_in_dim(spectral, lax.axis_index("chan") * local_chans, local_chans, 0)
    image = spec_local[:, 0][:, None, None] * model_full[0][None]
    for basis_idx in range(1, basis):
        image = image + spec_local[:, basis_idx][:, None, None] * model_full[basis_idx][None]
    image = image.astype(jnp.bfloat16)
    def with_dirty(cols):
        return jnp.concatenate([image, jnp.concatenate([cols[:, : row_count // 2], cols[:, row_count // 2 :]], axis=2)], axis=1)

    to_right = with_dirty(dirty[:, :, slot_width - HALF :])
    to_left = with_dirty(dirty[:, :, :HALF])
    left = from_behind(to_right, "sky", 1)
    right = from_behind(to_left, "sky", -1)

    taps = jnp.concatenate([psf_rows, psf_cols], axis=1)
    taps = jnp.pad(taps, ((0, 0), (0, 0), (0, LANES - TAPS)))
    piece_rows = row_count // chan_count
    ext = slot_width + 2 * HALF
    band_shapes = (
        jax.ShapeDtypeStruct((local_chans, ext, rank_count * slot_width), jnp.bfloat16),
        jax.ShapeDtypeStruct((local_chans, rank_count, row_count, row_count), jnp.bfloat16),
    )
    bands = pl.pallas_call(
        functools.partial(band_kernel, rank_count, local_chans, slot_width),
        out_shape=band_shapes * 2,
        in_specs=[vmem_spec()],
        out_specs=[vmem_spec()] * 4,
    )(taps)
    residual, partial_value = pl.pallas_call(
        functools.partial(main_kernel, rank_count, local_chans, sky_count),
        out_shape=(
            jax.ShapeDtypeStruct(dirty.shape, jnp.bfloat16),
            jax.ShapeDtypeStruct((chan_count, basis, piece_rows, slot_width), jnp.float32),
        ),
        grid=(local_chans,),
        in_specs=[smem_spec()] + [per_chan(a.shape) for a in (*bands, left, image, right, dirty)],
        out_specs=[
            per_chan(dirty.shape),
            pl.BlockSpec((chan_count, basis, piece_rows, slot_width), lambda c: (0, 0, 0, 0)),
        ],
    )(spectral, *bands, left, image, right, dirty)

    pieces = lax.all_to_all(partial_value, "chan", 0, 0, tiled=True)

    gram_rows = jnp.einsum("crt,cst->crs", psf_rows, psf_rows, precision=lax.Precision.HIGHEST)
    gram_cols = jnp.einsum("crt,cst->crs", psf_cols, psf_cols, precision=lax.Precision.HIGHEST)
    energy = jnp.sum(gram_rows * gram_cols, axis=(1, 2))
    curvature = jnp.sum(spectral * spectral * energy[:, None], axis=0)
    model_new = pl.pallas_call(
        update_kernel,
        out_shape=jax.ShapeDtypeStruct(model.shape, model.dtype),
        in_specs=[smem_spec(), vmem_spec(), vmem_spec()],
        out_specs=vmem_spec(),
    )(curvature, pieces, model)
    return (residual, model_new)


def solution(mesh):
    placed = (P("chan", None, "sky"), P(None, "chan", "sky"), P(), P(), P(), P())
    return jax.shard_map(
        body,
        mesh=mesh,
        in_specs=placed,
        out_specs=(P("chan", None, "sky"), P(None, "chan", "sky")),
        check_vma=False,
    )
```

```python
import functools

import jax
import jax.numpy as jnp
from jax import lax
from jax.experimental import pallas as pl
from jax.experimental.pallas import tpu as pltpu
from jax.sharding import PartitionSpec as P

TAPS = 129
HALF = (TAPS - 1) // 2
LANES = 512


def from_behind(value, axis, steps):
    count = lax.axis_size(axis)
    first, last = (max(0, -steps), min(count, count - steps))
    return lax.ppermute(value, axis, [(source, source + steps) for source in range(first, last)])


def col_band(w, slot):
    ext = slot + 2 * HALF
    spread = jnp.broadcast_to(w[:, :ext], (ext, ext))
    return pltpu.roll(spread, ext - 2 * HALF, 1, stride=1, stride_axis=0)[:, :slot]


def row_band(w, rows):
    spread = jnp.broadcast_to(w, (rows, LANES))
    return pltpu.roll(spread, LANES - HALF, 1, stride=1, stride_axis=0)[:, :rows]


def row_pass(row_ref, col_pass, rank_count, slot):
    total = None
    for r in range(rank_count):
        part = jnp.dot(
            row_ref[r], col_pass[:, r * slot : (r + 1) * slot], preferred_element_type=jnp.float32
        )
        total = part if total is None else total + part
    return total


def band_kernel(rank_count, local_chans, slot, taps_ref, colf_ref, rowf_ref, cola_ref, rowa_ref):
    rows = rowf_ref.shape[-1]
    first_chan = lax.axis_index("chan") * local_chans
    flip = (
        lax.broadcasted_iota(jnp.int32, (LANES // 2, LANES), 0)
        + lax.broadcasted_iota(jnp.int32, (LANES // 2, LANES), 1)
        == TAPS - 1
    ).astype(jnp.bfloat16)
    for c in range(local_chans):
        taps = taps_ref[first_chan + c].astype(jnp.bfloat16)
        rev = jnp.dot(taps[:, : LANES // 2], flip, preferred_element_type=jnp.float32)
        taps = taps.astype(jnp.float32)
        for r in range(rank_count):
            u, v = taps[r : r + 1], taps[rank_count + r : rank_count + r + 1]
            u_rev, v_rev = rev[r : r + 1], rev[rank_count + r : rank_count + r + 1]
            colf_ref[c, :, r * slot : (r + 1) * slot] = col_band(v_rev, slot).astype(jnp.bfloat16)
            cola_ref[c, :, r * slot : (r + 1) * slot] = col_band(v, slot).astype(jnp.bfloat16)
            rowf_ref[c, r] = row_band(u, rows).astype(jnp.bfloat16)
            rowa_ref[c, r] = row_band(u_rev, rows).astype(jnp.bfloat16)


def main_kernel(
    rank_count, local_chans, sky_count, spec_ref, colf_ref, rowf_ref, cola_ref, rowa_ref,
    left_ref, xc_ref, right_ref, dirty_ref, res_ref, part_ref,
):
    slot = xc_ref.shape[-1]
    rows = xc_ref.shape[0]
    pieces, basis, piece_rows, _ = part_ref.shape
    first_chan = lax.axis_index("chan") * local_chans
    sky_index = lax.axis_index("sky")
    lane = lax.broadcasted_iota(jnp.int32, (rows, slot), 1)
    step = pl.program_id(0)
    if True:
        xl, xc, xr = left_ref[:rows], xc_ref[...], right_ref[:rows]
        stacked = jnp.concatenate(
            [jnp.concatenate([xl, xc], axis=1), jnp.concatenate([xc, xr], axis=1)], axis=0
        )
        col_pass = jnp.dot(stacked, colf_ref[...], preferred_element_type=jnp.float32).astype(jnp.bfloat16)
        pred = None
        for r in range(rank_count):
            both = jnp.concatenate(
                [col_pass[:rows, r * slot : (r + 1) * slot], col_pass[rows:, r * slot : (r + 1) * slot]], axis=1
            )
            part = jnp.dot(rowf_ref[r], both, preferred_element_type=jnp.float32)
            pred = part if pred is None else pred + part
        pred_low, pred_high = pred[:, :slot], pred[:, slot:]
        pred_own = pltpu.roll(jnp.where(lane < HALF, pred_high, pred_low), HALF, 1)
        res_own = (dirty_ref[...].astype(jnp.float32) - pred_own).astype(jnp.bfloat16)
        res_ref[...] = res_own
        packed_l, packed_r = left_ref[rows:], right_ref[rows:]
        dl = jnp.concatenate([packed_l, pltpu.roll(packed_l, HALF, 1)], axis=0).astype(jnp.float32)
        dr = jnp.concatenate([pltpu.roll(packed_r, HALF, 1), packed_r], axis=0).astype(jnp.float32)
        halo_l = jnp.where(sky_index > 0, dl - pred_low, 0.0).astype(jnp.bfloat16)
        halo_r = jnp.where(sky_index < sky_count - 1, dr - pred_high, 0.0).astype(jnp.bfloat16)
        shifted = pltpu.roll(res_own, HALF, 1)
        res_low = jnp.where(lane < HALF, halo_l, shifted)
        res_high = jnp.where(lane < HALF, shifted, halo_r)
        adj_in = jnp.concatenate([res_low, res_high], axis=1)
        adj_pass = jnp.dot(adj_in, cola_ref[...], preferred_element_type=jnp.float32).astype(jnp.bfloat16)
        grad_chan = row_pass(rowa_ref, adj_pass, rank_count, slot)
        @pl.when(step == 0)
        def _():
            for j in range(pieces):
                block = grad_chan[j * piece_rows : (j + 1) * piece_rows]
                for b in range(basis):
                    part_ref[j, b] = spec_ref[first_chan, b] * block

        @pl.when(step > 0)
        def _():
            for j in range(pieces):
                block = grad_chan[j * piece_rows : (j + 1) * piece_rows]
                for b in range(basis):
                    part_ref[j, b] = part_ref[j, b] + spec_ref[first_chan + step, b] * block


def vmem_spec():
    return pl.BlockSpec(memory_space=pltpu.VMEM)


def per_chan(shape):
    return pl.BlockSpec((None,) + tuple(shape[1:]), lambda c: (c,) + (0,) * (len(shape) - 1))


def smem_spec():
    return pl.BlockSpec(memory_space=pltpu.SMEM)


def body(dirty, model, spectral, psf_rows, psf_cols, strip_width):
    local_chans, row_count, slot_width = dirty.shape
    basis = model.shape[0]
    rank_count = psf_rows.shape[1]
    chan_count = lax.axis_size("chan")
    sky_count = lax.axis_size("sky")

    model_full = lax.all_gather(model, "chan", axis=1, tiled=True)
    spec_local = lax.dynamic_slice_in_dim(spectral, lax.axis_index("chan") * local_chans, local_chans, 0)
    image = spec_local[:, 0][:, None, None] * model_full[0][None]
    for basis_idx in range(1, basis):
        image = image + spec_local[:, basis_idx][:, None, None] * model_full[basis_idx][None]
    image = image.astype(jnp.bfloat16)
    def with_dirty(cols):
        return jnp.concatenate([image, jnp.concatenate([cols[:, : row_count // 2], cols[:, row_count // 2 :]], axis=2)], axis=1)

    to_right = with_dirty(dirty[:, :, slot_width - HALF :])
    to_left = with_dirty(dirty[:, :, :HALF])
    left = from_behind(to_right, "sky", 1)
    right = from_behind(to_left, "sky", -1)

    taps = jnp.concatenate([psf_rows, psf_cols], axis=1)
    taps = jnp.pad(taps, ((0, 0), (0, 0), (0, LANES - TAPS)))
    piece_rows = row_count // chan_count
    ext = slot_width + 2 * HALF
    band_shapes = (
        jax.ShapeDtypeStruct((local_chans, ext, rank_count * slot_width), jnp.bfloat16),
        jax.ShapeDtypeStruct((local_chans, rank_count, row_count, row_count), jnp.bfloat16),
    )
    bands = pl.pallas_call(
        functools.partial(band_kernel, rank_count, local_chans, slot_width),
        out_shape=band_shapes * 2,
        in_specs=[vmem_spec()],
        out_specs=[vmem_spec()] * 4,
    )(taps)
    residual, partial_value = pl.pallas_call(
        functools.partial(main_kernel, rank_count, local_chans, sky_count),
        out_shape=(
            jax.ShapeDtypeStruct(dirty.shape, jnp.bfloat16),
            jax.ShapeDtypeStruct((chan_count, basis, piece_rows, slot_width), jnp.float32),
        ),
        grid=(local_chans,),
        in_specs=[smem_spec()] + [per_chan(a.shape) for a in (*bands, left, image, right, dirty)],
        out_specs=[
            per_chan(dirty.shape),
            pl.BlockSpec((chan_count, basis, piece_rows, slot_width), lambda c: (0, 0, 0, 0)),
        ],
    )(spectral, *bands, left, image, right, dirty)

    pieces = lax.all_to_all(partial_value, "chan", 0, 0, tiled=True)

    gram_rows = jnp.einsum("crt,cst->crs", psf_rows, psf_rows, precision=lax.Precision.HIGHEST)
    gram_cols = jnp.einsum("crt,cst->crs", psf_cols, psf_cols, precision=lax.Precision.HIGHEST)
    energy = jnp.sum(gram_rows * gram_cols, axis=(1, 2))
    curvature = jnp.sum(spectral * spectral * energy[:, None], axis=0)
    model_new = model + pieces.sum(0) / curvature[:, None, None]
    return (residual, model_new)


def solution(mesh):
    placed = (P("chan", None, "sky"), P(None, "chan", "sky"), P(), P(), P(), P())
    return jax.shard_map(
        body,
        mesh=mesh,
        in_specs=placed,
        out_specs=(P("chan", None, "sky"), P(None, "chan", "sky")),
        check_vma=False,
    )
```

```python
import functools

import jax
import jax.numpy as jnp
from jax import lax
from jax.experimental import pallas as pl
from jax.experimental.pallas import tpu as pltpu
from jax.sharding import PartitionSpec as P

TAPS = 129
HALF = (TAPS - 1) // 2
LANES = 512


def from_behind(value, axis, steps):
    count = lax.axis_size(axis)
    first, last = (max(0, -steps), min(count, count - steps))
    return lax.ppermute(value, axis, [(source, source + steps) for source in range(first, last)])


def col_band(w, slot):
    ext = slot + 2 * HALF
    spread = jnp.broadcast_to(w[:, :ext], (ext, ext))
    return pltpu.roll(spread, ext - 2 * HALF, 1, stride=1, stride_axis=0)[:, :slot]


def row_band(w, rows):
    spread = jnp.broadcast_to(w, (rows, LANES))
    return pltpu.roll(spread, LANES - HALF, 1, stride=1, stride_axis=0)[:, :rows]


def row_pass(row_ref, col_pass, rank_count, slot):
    total = None
    for r in range(rank_count):
        part = jnp.dot(
            row_ref[r], col_pass[:, r * slot : (r + 1) * slot], preferred_element_type=jnp.float32
        )
        total = part if total is None else total + part
    return total


def band_kernel(rank_count, local_chans, slot, taps_ref, colf_ref, rowf_ref, cola_ref, rowa_ref):
    rows = rowf_ref.shape[-1]
    first_chan = lax.axis_index("chan") * local_chans
    flip = (
        lax.broadcasted_iota(jnp.int32, (LANES // 2, LANES), 0)
        + lax.broadcasted_iota(jnp.int32, (LANES // 2, LANES), 1)
        == TAPS - 1
    ).astype(jnp.bfloat16)
    for c in range(local_chans):
        taps = taps_ref[first_chan + c].astype(jnp.bfloat16)
        rev = jnp.dot(taps[:, : LANES // 2], flip, preferred_element_type=jnp.float32)
        taps = taps.astype(jnp.float32)
        for r in range(rank_count):
            u, v = taps[r : r + 1], taps[rank_count + r : rank_count + r + 1]
            u_rev, v_rev = rev[r : r + 1], rev[rank_count + r : rank_count + r + 1]
            colf_ref[c, :, r * slot : (r + 1) * slot] = col_band(v_rev, slot).astype(jnp.bfloat16)
            cola_ref[c, :, r * slot : (r + 1) * slot] = col_band(v, slot).astype(jnp.bfloat16)
            rowf_ref[c, r] = row_band(u, rows).astype(jnp.bfloat16)
            rowa_ref[c, r] = row_band(u_rev, rows).astype(jnp.bfloat16)


def main_kernel(
    rank_count, local_chans, sky_count, spec_ref, colf_ref, rowf_ref, cola_ref, rowa_ref,
    left_ref, xc_ref, right_ref, dirty_ref, res_ref, part_ref,
):
    slot = xc_ref.shape[-1]
    rows = xc_ref.shape[0]
    pieces, basis, piece_rows, _ = part_ref.shape
    first_chan = lax.axis_index("chan") * local_chans
    sky_index = lax.axis_index("sky")
    lane = lax.broadcasted_iota(jnp.int32, (rows, slot), 1)
    step = pl.program_id(0)
    if True:
        xl, xc, xr = left_ref[:rows], xc_ref[...], right_ref[:rows]
        stacked = jnp.concatenate(
            [jnp.concatenate([xl, xc], axis=1), jnp.concatenate([xc, xr], axis=1)], axis=0
        )
        col_pass = jnp.dot(stacked, colf_ref[...], preferred_element_type=jnp.float32).astype(jnp.bfloat16)
        pred = None
        for r in range(rank_count):
            both = jnp.concatenate(
                [col_pass[:rows, r * slot : (r + 1) * slot], col_pass[rows:, r * slot : (r + 1) * slot]], axis=1
            )
            part = jnp.dot(rowf_ref[r], both, preferred_element_type=jnp.float32)
            pred = part if pred is None else pred + part
        pred_low, pred_high = pred[:, :slot], pred[:, slot:]
        pred_own = pltpu.roll(jnp.where(lane < HALF, pred_high, pred_low), HALF, 1)
        res_own = (dirty_ref[...].astype(jnp.float32) - pred_own).astype(jnp.bfloat16)
        res_ref[...] = res_own
        packed_l, packed_r = left_ref[rows:], right_ref[rows:]
        dl = jnp.concatenate([packed_l, pltpu.roll(packed_l, HALF, 1)], axis=0).astype(jnp.float32)
        dr = jnp.concatenate([pltpu.roll(packed_r, HALF, 1), packed_r], axis=0).astype(jnp.float32)
        halo_l = jnp.where(sky_index > 0, dl - pred_low, 0.0).astype(jnp.bfloat16)
        halo_r = jnp.where(sky_index < sky_count - 1, dr - pred_high, 0.0).astype(jnp.bfloat16)
        shifted = pltpu.roll(res_own, HALF, 1)
        res_low = jnp.where(lane < HALF, halo_l, shifted)
        res_high = jnp.where(lane < HALF, shifted, halo_r)
        adj_in = jnp.concatenate([res_low, res_high], axis=1)
        adj_pass = jnp.dot(adj_in, cola_ref[...], preferred_element_type=jnp.float32).astype(jnp.bfloat16)
        grad_chan = row_pass(rowa_ref, adj_pass, rank_count, slot)
        @pl.when(step == 0)
        def _():
            for j in range(pieces):
                block = grad_chan[j * piece_rows : (j + 1) * piece_rows]
                for b in range(basis):
                    part_ref[j, b] = spec_ref[first_chan, b] * block

        @pl.when(step > 0)
        def _():
            for j in range(pieces):
                block = grad_chan[j * piece_rows : (j + 1) * piece_rows]
                for b in range(basis):
                    part_ref[j, b] = part_ref[j, b] + spec_ref[first_chan + step, b] * block


def vmem_spec():
    return pl.BlockSpec(memory_space=pltpu.VMEM)


def per_chan(shape):
    return pl.BlockSpec((None,) + tuple(shape[1:]), lambda c: (c,) + (0,) * (len(shape) - 1))


def smem_spec():
    return pl.BlockSpec(memory_space=pltpu.SMEM)


def body(dirty, model, spectral, psf_rows, psf_cols, strip_width):
    local_chans, row_count, slot_width = dirty.shape
    basis = model.shape[0]
    rank_count = psf_rows.shape[1]
    chan_count = lax.axis_size("chan")
    sky_count = lax.axis_size("sky")

    model_full = lax.all_gather(model, "chan", axis=1, tiled=True)
    spec_local = lax.dynamic_slice_in_dim(spectral, lax.axis_index("chan") * local_chans, local_chans, 0)
    image = spec_local[:, 0][:, None, None] * model_full[0][None]
    for basis_idx in range(1, basis):
        image = image + spec_local[:, basis_idx][:, None, None] * model_full[basis_idx][None]
    image = image.astype(jnp.bfloat16)
    def with_dirty(cols):
        return jnp.concatenate([image, jnp.concatenate([cols[:, : row_count // 2], cols[:, row_count // 2 :]], axis=2)], axis=1)

    to_right = with_dirty(dirty[:, :, slot_width - HALF :])
    to_left = with_dirty(dirty[:, :, :HALF])
    left = from_behind(to_right, "sky", 1)
    right = from_behind(to_left, "sky", -1)

    taps = jnp.concatenate([psf_rows, psf_cols], axis=1)
    taps = jnp.pad(taps, ((0, 0), (0, 0), (0, LANES - TAPS)))
    piece_rows = row_count // chan_count
    ext = slot_width + 2 * HALF
    band_shapes = (
        jax.ShapeDtypeStruct((local_chans, ext, rank_count * slot_width), jnp.bfloat16),
        jax.ShapeDtypeStruct((local_chans, rank_count, row_count, row_count), jnp.bfloat16),
    )
    bands = pl.pallas_call(
        functools.partial(band_kernel, rank_count, local_chans, slot_width),
        out_shape=band_shapes * 2,
        in_specs=[vmem_spec()],
        out_specs=[vmem_spec()] * 4,
    )(taps)
    residual, partial_value = pl.pallas_call(
        functools.partial(main_kernel, rank_count, local_chans, sky_count),
        out_shape=(
            jax.ShapeDtypeStruct(dirty.shape, jnp.bfloat16),
            jax.ShapeDtypeStruct((chan_count, basis, piece_rows, slot_width), jnp.float32),
        ),
        grid=(local_chans,),
        in_specs=[smem_spec()] + [per_chan(a.shape) for a in (*bands, left, image, right, dirty)],
        out_specs=[
            per_chan(dirty.shape),
            pl.BlockSpec((chan_count, basis, piece_rows, slot_width), lambda c: (0, 0, 0, 0)),
        ],
    )(spectral, *bands, left, image, right, dirty)

    pieces = lax.all_to_all(partial_value, "chan", 0, 0, tiled=True)

    gram_rows = jnp.einsum("crt,cst->crs", psf_rows, psf_rows, precision=lax.Precision.HIGHEST)
    gram_cols = jnp.einsum("crt,cst->crs", psf_cols, psf_cols, precision=lax.Precision.HIGHEST)
    energy = jnp.sum(gram_rows * gram_cols, axis=(1, 2))
    curvature = jnp.sum(spectral * spectral * energy[:, None], axis=0)
    own_rows = lax.dynamic_slice_in_dim(model_full, lax.axis_index("chan") * piece_rows, piece_rows, 1)
    model_new = own_rows + pieces.sum(0) / curvature[:, None, None]
    return (residual, model_new)


def solution(mesh):
    placed = (P("chan", None, "sky"), P(None, "chan", "sky"), P(), P(), P(), P())
    return jax.shard_map(
        body,
        mesh=mesh,
        in_specs=placed,
        out_specs=(P("chan", None, "sky"), P(None, "chan", "sky")),
        check_vma=False,
    )
```

```python
import functools

import jax
import jax.numpy as jnp
from jax import lax
from jax.experimental import pallas as pl
from jax.experimental.pallas import tpu as pltpu
from jax.sharding import PartitionSpec as P

TAPS = 129
HALF = (TAPS - 1) // 2
LANES = 512


def from_behind(value, axis, steps):
    count = lax.axis_size(axis)
    first, last = (max(0, -steps), min(count, count - steps))
    return lax.ppermute(value, axis, [(source, source + steps) for source in range(first, last)])


def col_band(w, slot):
    ext = slot + 2 * HALF
    spread = jnp.broadcast_to(w[:, :ext], (ext, ext))
    return pltpu.roll(spread, ext - 2 * HALF, 1, stride=1, stride_axis=0)[:, :slot]


def row_band(w, rows):
    spread = jnp.broadcast_to(w, (rows, LANES))
    return pltpu.roll(spread, LANES - HALF, 1, stride=1, stride_axis=0)[:, :rows]


def row_pass(row_ref, col_pass, rank_count, slot):
    total = None
    for r in range(rank_count):
        part = jnp.dot(
            row_ref[r], col_pass[:, r * slot : (r + 1) * slot], preferred_element_type=jnp.float32
        )
        total = part if total is None else total + part
    return total


def band_kernel(rank_count, local_chans, slot, taps_ref, colf_ref, rowf_ref, cola_ref, rowa_ref):
    rows = rowf_ref.shape[-1]
    first_chan = lax.axis_index("chan") * local_chans
    flip = (
        lax.broadcasted_iota(jnp.int32, (LANES // 2, LANES), 0)
        + lax.broadcasted_iota(jnp.int32, (LANES // 2, LANES), 1)
        == TAPS - 1
    ).astype(jnp.bfloat16)
    for c in range(local_chans):
        taps = taps_ref[first_chan + c].astype(jnp.bfloat16)
        rev = jnp.dot(taps[:, : LANES // 2], flip, preferred_element_type=jnp.float32)
        taps = taps.astype(jnp.float32)
        for r in range(rank_count):
            u, v = taps[r : r + 1], taps[rank_count + r : rank_count + r + 1]
            u_rev, v_rev = rev[r : r + 1], rev[rank_count + r : rank_count + r + 1]
            colf_ref[c, :, r * slot : (r + 1) * slot] = col_band(v_rev, slot).astype(jnp.bfloat16)
            cola_ref[c, :, r * slot : (r + 1) * slot] = col_band(v, slot).astype(jnp.bfloat16)
            rowf_ref[c, r] = row_band(u, rows).astype(jnp.bfloat16)
            rowa_ref[c, r] = row_band(u_rev, rows).astype(jnp.bfloat16)


def main_kernel(
    rank_count, local_chans, sky_count, spec_ref, colf_ref, rowf_ref, cola_ref, rowa_ref,
    left_ref, xc_ref, right_ref, dirty_ref, res_ref, part_ref,
):
    slot = xc_ref.shape[-1]
    rows = xc_ref.shape[0]
    pieces, basis, piece_rows, _ = part_ref.shape
    first_chan = lax.axis_index("chan") * local_chans
    sky_index = lax.axis_index("sky")
    lane = lax.broadcasted_iota(jnp.int32, (rows, slot), 1)
    step = pl.program_id(0)
    if True:
        xl, xc, xr = left_ref[:rows], xc_ref[...], right_ref[:rows]
        stacked = jnp.concatenate(
            [jnp.concatenate([xl, xc], axis=1), jnp.concatenate([xc, xr], axis=1)], axis=0
        )
        col_pass = jnp.dot(stacked, colf_ref[...], preferred_element_type=jnp.float32).astype(jnp.bfloat16)
        pred = None
        for r in range(rank_count):
            both = jnp.concatenate(
                [col_pass[:rows, r * slot : (r + 1) * slot], col_pass[rows:, r * slot : (r + 1) * slot]], axis=1
            )
            part = jnp.dot(rowf_ref[r], both, preferred_element_type=jnp.float32)
            pred = part if pred is None else pred + part
        pred_low, pred_high = pred[:, :slot], pred[:, slot:]
        pred_own = pltpu.roll(jnp.where(lane < HALF, pred_high, pred_low), HALF, 1)
        res_own = (dirty_ref[...].astype(jnp.float32) - pred_own).astype(jnp.bfloat16)
        res_ref[...] = res_own
        packed_l, packed_r = left_ref[rows:], right_ref[rows:]
        dl = jnp.concatenate([packed_l, pltpu.roll(packed_l, HALF, 1)], axis=0).astype(jnp.float32)
        dr = jnp.concatenate([pltpu.roll(packed_r, HALF, 1), packed_r], axis=0).astype(jnp.float32)
        halo_l = jnp.where(sky_index > 0, dl - pred_low, 0.0).astype(jnp.bfloat16)
        halo_r = jnp.where(sky_index < sky_count - 1, dr - pred_high, 0.0).astype(jnp.bfloat16)
        shifted = pltpu.roll(res_own, HALF, 1)
        res_low = jnp.where(lane < HALF, halo_l, shifted)
        res_high = jnp.where(lane < HALF, shifted, halo_r)
        adj_in = jnp.concatenate([res_low, res_high], axis=1)
        adj_pass = jnp.dot(adj_in, cola_ref[...], preferred_element_type=jnp.float32).astype(jnp.bfloat16)
        grad_chan = row_pass(rowa_ref, adj_pass, rank_count, slot)
        @pl.when(step == 0)
        def _():
            for j in range(pieces):
                block = grad_chan[j * piece_rows : (j + 1) * piece_rows]
                for b in range(basis):
                    part_ref[j, b] = spec_ref[first_chan, b] * block

        @pl.when(step > 0)
        def _():
            for j in range(pieces):
                block = grad_chan[j * piece_rows : (j + 1) * piece_rows]
                for b in range(basis):
                    part_ref[j, b] = part_ref[j, b] + spec_ref[first_chan + step, b] * block


def vmem_spec():
    return pl.BlockSpec(memory_space=pltpu.VMEM)


def per_chan(shape):
    return pl.BlockSpec((None,) + tuple(shape[1:]), lambda c: (c,) + (0,) * (len(shape) - 1))


def smem_spec():
    return pl.BlockSpec(memory_space=pltpu.SMEM)


def body(dirty, model, spectral, psf_rows, psf_cols, strip_width):
    local_chans, row_count, slot_width = dirty.shape
    basis = model.shape[0]
    rank_count = psf_rows.shape[1]
    chan_count = lax.axis_size("chan")
    sky_count = lax.axis_size("sky")

    def packed(cols):
        return jnp.concatenate([cols[:, : row_count // 2], cols[:, row_count // 2 :]], axis=2)

    model, dirty_r, dirty_l = lax.optimization_barrier(
        (model, packed(dirty[:, :, slot_width - HALF :]), packed(dirty[:, :, :HALF]))
    )
    model_full = lax.all_gather(model, "chan", axis=1, tiled=True)
    spec_local = lax.dynamic_slice_in_dim(spectral, lax.axis_index("chan") * local_chans, local_chans, 0)
    image = spec_local[:, 0][:, None, None] * model_full[0][None]
    for basis_idx in range(1, basis):
        image = image + spec_local[:, basis_idx][:, None, None] * model_full[basis_idx][None]
    image = image.astype(jnp.bfloat16)
    to_right = jnp.concatenate([image, dirty_r], axis=1)
    to_left = jnp.concatenate([image, dirty_l], axis=1)
    left = from_behind(to_right, "sky", 1)
    right = from_behind(to_left, "sky", -1)

    taps = jnp.concatenate([psf_rows, psf_cols], axis=1)
    taps = jnp.pad(taps, ((0, 0), (0, 0), (0, LANES - TAPS)))
    piece_rows = row_count // chan_count
    ext = slot_width + 2 * HALF
    band_shapes = (
        jax.ShapeDtypeStruct((local_chans, ext, rank_count * slot_width), jnp.bfloat16),
        jax.ShapeDtypeStruct((local_chans, rank_count, row_count, row_count), jnp.bfloat16),
    )
    bands = pl.pallas_call(
        functools.partial(band_kernel, rank_count, local_chans, slot_width),
        out_shape=band_shapes * 2,
        in_specs=[vmem_spec()],
        out_specs=[vmem_spec()] * 4,
    )(taps)
    residual, partial_value = pl.pallas_call(
        functools.partial(main_kernel, rank_count, local_chans, sky_count),
        out_shape=(
            jax.ShapeDtypeStruct(dirty.shape, jnp.bfloat16),
            jax.ShapeDtypeStruct((chan_count, basis, piece_rows, slot_width), jnp.float32),
        ),
        grid=(local_chans,),
        in_specs=[smem_spec()] + [per_chan(a.shape) for a in (*bands, left, image, right, dirty)],
        out_specs=[
            per_chan(dirty.shape),
            pl.BlockSpec((chan_count, basis, piece_rows, slot_width), lambda c: (0, 0, 0, 0)),
        ],
    )(spectral, *bands, left, image, right, dirty)

    pieces = lax.all_to_all(partial_value, "chan", 0, 0, tiled=True)

    gram_rows = jnp.einsum("crt,cst->crs", psf_rows, psf_rows, precision=lax.Precision.HIGHEST)
    gram_cols = jnp.einsum("crt,cst->crs", psf_cols, psf_cols, precision=lax.Precision.HIGHEST)
    energy = jnp.sum(gram_rows * gram_cols, axis=(1, 2))
    curvature = jnp.sum(spectral * spectral * energy[:, None], axis=0)
    own_rows = lax.dynamic_slice_in_dim(model_full, lax.axis_index("chan") * piece_rows, piece_rows, 1)
    model_new = own_rows + pieces.sum(0) / curvature[:, None, None]
    return (residual, model_new)


def solution(mesh):
    placed = (P("chan", None, "sky"), P(None, "chan", "sky"), P(), P(), P(), P())
    return jax.shard_map(
        body,
        mesh=mesh,
        in_specs=placed,
        out_specs=(P("chan", None, "sky"), P(None, "chan", "sky")),
        check_vma=False,
    )
```

```python
import functools

import jax
import jax.numpy as jnp
from jax import lax
from jax.experimental import pallas as pl
from jax.experimental.pallas import tpu as pltpu
from jax.sharding import PartitionSpec as P

TAPS = 129
HALF = (TAPS - 1) // 2
LANES = 512


def from_behind(value, axis, steps):
    count = lax.axis_size(axis)
    first, last = (max(0, -steps), min(count, count - steps))
    return lax.ppermute(value, axis, [(source, source + steps) for source in range(first, last)])


def col_band(w, slot):
    ext = slot + 2 * HALF
    spread = jnp.broadcast_to(w[:, :ext], (ext, ext))
    return pltpu.roll(spread, ext - 2 * HALF, 1, stride=1, stride_axis=0)[:, :slot]


def row_band(w, rows):
    spread = jnp.broadcast_to(w, (rows, LANES))
    return pltpu.roll(spread, LANES - HALF, 1, stride=1, stride_axis=0)[:, :rows]


def row_pass(row_ref, col_pass, rank_count, slot):
    total = None
    for r in range(rank_count):
        part = jnp.dot(
            row_ref[r], col_pass[:, r * slot : (r + 1) * slot], preferred_element_type=jnp.float32
        )
        total = part if total is None else total + part
    return total


def band_kernel(rank_count, local_chans, slot, taps_ref, colf_ref, rowf_ref, cola_ref, rowa_ref):
    rows = rowf_ref.shape[-1]
    first_chan = lax.axis_index("chan") * local_chans
    flip = (
        lax.broadcasted_iota(jnp.int32, (LANES // 2, LANES), 0)
        + lax.broadcasted_iota(jnp.int32, (LANES // 2, LANES), 1)
        == TAPS - 1
    ).astype(jnp.bfloat16)
    for c in range(local_chans):
        taps = taps_ref[first_chan + c].astype(jnp.bfloat16)
        rev = jnp.dot(taps[:, : LANES // 2], flip, preferred_element_type=jnp.float32)
        taps = taps.astype(jnp.float32)
        for r in range(rank_count):
            u, v = taps[r : r + 1], taps[rank_count + r : rank_count + r + 1]
            u_rev, v_rev = rev[r : r + 1], rev[rank_count + r : rank_count + r + 1]
            colf_ref[c, :, r * slot : (r + 1) * slot] = col_band(v_rev, slot).astype(jnp.bfloat16)
            cola_ref[c, :, r * slot : (r + 1) * slot] = col_band(v, slot).astype(jnp.bfloat16)
            rowf_ref[c, r] = row_band(u, rows).astype(jnp.bfloat16)
            rowa_ref[c, r] = row_band(u_rev, rows).astype(jnp.bfloat16)


def main_kernel(
    rank_count, local_chans, sky_count, spec_ref, colf_ref, rowf_ref, cola_ref, rowa_ref,
    left_ref, xc_ref, right_ref, dirty_ref, res_ref, part_ref,
):
    slot = xc_ref.shape[-1]
    rows = dirty_ref.shape[0]
    pieces, basis, piece_rows, _ = part_ref.shape
    first_chan = lax.axis_index("chan") * local_chans
    sky_index = lax.axis_index("sky")
    lane = lax.broadcasted_iota(jnp.int32, (rows, slot), 1)
    step = pl.program_id(0)
    if True:
        xl, xc, xr = left_ref[:rows], xc_ref[:rows], right_ref[:rows]
        stacked = jnp.concatenate(
            [jnp.concatenate([xl, xc], axis=1), jnp.concatenate([xc, xr], axis=1)], axis=0
        )
        col_pass = jnp.dot(stacked, colf_ref[...], preferred_element_type=jnp.float32).astype(jnp.bfloat16)
        pred = None
        for r in range(rank_count):
            both = jnp.concatenate(
                [col_pass[:rows, r * slot : (r + 1) * slot], col_pass[rows:, r * slot : (r + 1) * slot]], axis=1
            )
            part = jnp.dot(rowf_ref[r], both, preferred_element_type=jnp.float32)
            pred = part if pred is None else pred + part
        pred_low, pred_high = pred[:, :slot], pred[:, slot:]
        pred_own = pltpu.roll(jnp.where(lane < HALF, pred_high, pred_low), HALF, 1)
        res_own = (dirty_ref[...].astype(jnp.float32) - pred_own).astype(jnp.bfloat16)
        res_ref[...] = res_own
        packed_l, packed_r = left_ref[rows:], right_ref[rows:]
        dl = jnp.concatenate([packed_l, pltpu.roll(packed_l, HALF, 1)], axis=0).astype(jnp.float32)
        dr = jnp.concatenate([pltpu.roll(packed_r, HALF, 1), packed_r], axis=0).astype(jnp.float32)
        halo_l = jnp.where(sky_index > 0, dl - pred_low, 0.0).astype(jnp.bfloat16)
        halo_r = jnp.where(sky_index < sky_count - 1, dr - pred_high, 0.0).astype(jnp.bfloat16)
        shifted = pltpu.roll(res_own, HALF, 1)
        res_low = jnp.where(lane < HALF, halo_l, shifted)
        res_high = jnp.where(lane < HALF, shifted, halo_r)
        adj_in = jnp.concatenate([res_low, res_high], axis=1)
        adj_pass = jnp.dot(adj_in, cola_ref[...], preferred_element_type=jnp.float32).astype(jnp.bfloat16)
        grad_chan = row_pass(rowa_ref, adj_pass, rank_count, slot)
        @pl.when(step == 0)
        def _():
            for j in range(pieces):
                block = grad_chan[j * piece_rows : (j + 1) * piece_rows]
                for b in range(basis):
                    part_ref[j, b] = spec_ref[first_chan, b] * block

        @pl.when(step > 0)
        def _():
            for j in range(pieces):
                block = grad_chan[j * piece_rows : (j + 1) * piece_rows]
                for b in range(basis):
                    part_ref[j, b] = part_ref[j, b] + spec_ref[first_chan + step, b] * block


def vmem_spec():
    return pl.BlockSpec(memory_space=pltpu.VMEM)


def per_chan(shape):
    return pl.BlockSpec((None,) + tuple(shape[1:]), lambda c: (c,) + (0,) * (len(shape) - 1))


def smem_spec():
    return pl.BlockSpec(memory_space=pltpu.SMEM)


def body(dirty, model, spectral, psf_rows, psf_cols, strip_width):
    local_chans, row_count, slot_width = dirty.shape
    basis = model.shape[0]
    rank_count = psf_rows.shape[1]
    chan_count = lax.axis_size("chan")
    sky_count = lax.axis_size("sky")

    model_full = lax.all_gather(model, "chan", axis=1, tiled=True)
    spec_local = lax.dynamic_slice_in_dim(spectral, lax.axis_index("chan") * local_chans, local_chans, 0)
    image = spec_local[:, 0][:, None, None] * model_full[0][None]
    for basis_idx in range(1, basis):
        image = image + spec_local[:, basis_idx][:, None, None] * model_full[basis_idx][None]
    image = image.astype(jnp.bfloat16)
    def with_dirty(cols):
        return jnp.concatenate([image, jnp.concatenate([cols[:, : row_count // 2], cols[:, row_count // 2 :]], axis=2)], axis=1)

    to_right = with_dirty(dirty[:, :, slot_width - HALF :])
    to_left = with_dirty(dirty[:, :, :HALF])
    left = from_behind(to_right, "sky", 1)
    right = from_behind(to_left, "sky", -1)

    taps = jnp.concatenate([psf_rows, psf_cols], axis=1)
    taps = jnp.pad(taps, ((0, 0), (0, 0), (0, LANES - TAPS)))
    piece_rows = row_count // chan_count
    ext = slot_width + 2 * HALF
    band_shapes = (
        jax.ShapeDtypeStruct((local_chans, ext, rank_count * slot_width), jnp.bfloat16),
        jax.ShapeDtypeStruct((local_chans, rank_count, row_count, row_count), jnp.bfloat16),
    )
    bands = pl.pallas_call(
        functools.partial(band_kernel, rank_count, local_chans, slot_width),
        out_shape=band_shapes * 2,
        in_specs=[vmem_spec()],
        out_specs=[vmem_spec()] * 4,
    )(taps)
    residual, partial_value = pl.pallas_call(
        functools.partial(main_kernel, rank_count, local_chans, sky_count),
        out_shape=(
            jax.ShapeDtypeStruct(dirty.shape, jnp.bfloat16),
            jax.ShapeDtypeStruct((chan_count, basis, piece_rows, slot_width), jnp.float32),
        ),
        grid=(local_chans,),
        in_specs=[smem_spec()] + [per_chan(a.shape) for a in (*bands, left, image, right, dirty)],
        out_specs=[
            per_chan(dirty.shape),
            pl.BlockSpec((chan_count, basis, piece_rows, slot_width), lambda c: (0, 0, 0, 0)),
        ],
    )(spectral, *bands, left, to_right, right, dirty)

    pieces = lax.all_to_all(partial_value, "chan", 0, 0, tiled=True)

    gram_rows = jnp.einsum("crt,cst->crs", psf_rows, psf_rows, precision=lax.Precision.HIGHEST)
    gram_cols = jnp.einsum("crt,cst->crs", psf_cols, psf_cols, precision=lax.Precision.HIGHEST)
    energy = jnp.sum(gram_rows * gram_cols, axis=(1, 2))
    curvature = jnp.sum(spectral * spectral * energy[:, None], axis=0)
    own_rows = lax.dynamic_slice_in_dim(model_full, lax.axis_index("chan") * piece_rows, piece_rows, 1)
    model_new = own_rows + pieces.sum(0) / curvature[:, None, None]
    return (residual, model_new)


def solution(mesh):
    placed = (P("chan", None, "sky"), P(None, "chan", "sky"), P(), P(), P(), P())
    return jax.shard_map(
        body,
        mesh=mesh,
        in_specs=placed,
        out_specs=(P("chan", None, "sky"), P(None, "chan", "sky")),
        check_vma=False,
    )
```

```python
import functools

import jax
import jax.numpy as jnp
from jax import lax
from jax.experimental import pallas as pl
from jax.experimental.pallas import tpu as pltpu
from jax.sharding import PartitionSpec as P

TAPS = 129
HALF = (TAPS - 1) // 2
LANES = 512


def from_behind(value, axis, steps):
    count = lax.axis_size(axis)
    first, last = (max(0, -steps), min(count, count - steps))
    return lax.ppermute(value, axis, [(source, source + steps) for source in range(first, last)])


def col_band(w, slot):
    ext = slot + 2 * HALF
    spread = jnp.broadcast_to(w[:, :ext], (ext, ext))
    return pltpu.roll(spread, ext - 2 * HALF, 1, stride=1, stride_axis=0)[:, :slot]


def row_band(w, rows):
    spread = jnp.broadcast_to(w, (rows, LANES))
    return pltpu.roll(spread, LANES - HALF, 1, stride=1, stride_axis=0)[:, :rows]


def row_pass(row_ref, col_pass, rank_count, slot):
    total = None
    for r in range(rank_count):
        part = jnp.dot(
            row_ref[r], col_pass[:, r * slot : (r + 1) * slot], preferred_element_type=jnp.float32
        )
        total = part if total is None else total + part
    return total


def band_kernel(rank_count, local_chans, slot, taps_ref, colf_ref, rowf_ref, cola_ref, rowa_ref):
    rows = rowf_ref.shape[-1]
    first_chan = lax.axis_index("chan") * local_chans
    flip = (
        lax.broadcasted_iota(jnp.int32, (LANES // 2, LANES), 0)
        + lax.broadcasted_iota(jnp.int32, (LANES // 2, LANES), 1)
        == TAPS - 1
    ).astype(jnp.bfloat16)
    for c in range(local_chans):
        taps = taps_ref[first_chan + c].astype(jnp.bfloat16)
        rev = jnp.dot(taps[:, : LANES // 2], flip, preferred_element_type=jnp.float32)
        taps = taps.astype(jnp.float32)
        for r in range(rank_count):
            u, v = taps[r : r + 1], taps[rank_count + r : rank_count + r + 1]
            u_rev, v_rev = rev[r : r + 1], rev[rank_count + r : rank_count + r + 1]
            colf_ref[c, :, r * slot : (r + 1) * slot] = col_band(v_rev, slot).astype(jnp.bfloat16)
            cola_ref[c, :, r * slot : (r + 1) * slot] = col_band(v, slot).astype(jnp.bfloat16)
            rowf_ref[c, r] = row_band(u, rows).astype(jnp.bfloat16)
            rowa_ref[c, r] = row_band(u_rev, rows).astype(jnp.bfloat16)


def main_kernel(
    rank_count, local_chans, sky_count, spec_ref, colf_ref, rowf_ref, cola_ref, rowa_ref,
    left_ref, xc_ref, right_ref, dirty_ref, res_ref, part_ref,
):
    slot = xc_ref.shape[-1]
    rows = dirty_ref.shape[0]
    pieces, basis, piece_rows, _ = part_ref.shape
    first_chan = lax.axis_index("chan") * local_chans
    sky_index = lax.axis_index("sky")
    lane = lax.broadcasted_iota(jnp.int32, (rows, slot), 1)
    step = pl.program_id(0)
    if True:
        xl, xc, xr = left_ref[:rows], xc_ref[:rows], right_ref[:rows]
        stacked = jnp.concatenate(
            [jnp.concatenate([xl, xc], axis=1), jnp.concatenate([xc, xr], axis=1)], axis=0
        )
        col_pass = jnp.dot(stacked, colf_ref[...], preferred_element_type=jnp.float32).astype(jnp.bfloat16)
        pred = None
        for r in range(rank_count):
            both = jnp.concatenate(
                [col_pass[:rows, r * slot : (r + 1) * slot], col_pass[rows:, r * slot : (r + 1) * slot]], axis=1
            )
            part = jnp.dot(rowf_ref[r], both, preferred_element_type=jnp.float32)
            pred = part if pred is None else pred + part
        pred_low, pred_high = pred[:, :slot], pred[:, slot:]
        pred_own = pltpu.roll(jnp.where(lane < HALF, pred_high, pred_low), HALF, 1)
        res_own = (dirty_ref[...].astype(jnp.float32) - pred_own).astype(jnp.bfloat16)
        res_ref[...] = res_own
        packed_l, packed_r = left_ref[rows:], right_ref[rows:]
        dl = jnp.concatenate([packed_l, pltpu.roll(packed_l, HALF, 1)], axis=0).astype(jnp.float32)
        dr = jnp.concatenate([pltpu.roll(packed_r, HALF, 1), packed_r], axis=0).astype(jnp.float32)
        halo_l = jnp.where(sky_index > 0, dl - pred_low, 0.0).astype(jnp.bfloat16)
        halo_r = jnp.where(sky_index < sky_count - 1, dr - pred_high, 0.0).astype(jnp.bfloat16)
        shifted = pltpu.roll(res_own, HALF, 1)
        res_low = jnp.where(lane < HALF, halo_l, shifted)
        res_high = jnp.where(lane < HALF, shifted, halo_r)
        adj_in = jnp.concatenate([res_low, res_high], axis=1)
        adj_pass = jnp.dot(adj_in, cola_ref[...], preferred_element_type=jnp.float32).astype(jnp.bfloat16)
        grad_chan = row_pass(rowa_ref, adj_pass, rank_count, slot)
        @pl.when(step == 0)
        def _():
            for j in range(pieces):
                block = grad_chan[j * piece_rows : (j + 1) * piece_rows]
                for b in range(basis):
                    part_ref[j, b] = spec_ref[first_chan, b] * block

        @pl.when(step > 0)
        def _():
            for j in range(pieces):
                block = grad_chan[j * piece_rows : (j + 1) * piece_rows]
                for b in range(basis):
                    part_ref[j, b] = part_ref[j, b] + spec_ref[first_chan + step, b] * block


def vmem_spec():
    return pl.BlockSpec(memory_space=pltpu.VMEM)


def per_chan(shape):
    return pl.BlockSpec((None,) + tuple(shape[1:]), lambda c: (c,) + (0,) * (len(shape) - 1))


def smem_spec():
    return pl.BlockSpec(memory_space=pltpu.SMEM)


def body(dirty, model, spectral, psf_rows, psf_cols, strip_width):
    local_chans, row_count, slot_width = dirty.shape
    basis = model.shape[0]
    rank_count = psf_rows.shape[1]
    chan_count = lax.axis_size("chan")
    sky_count = lax.axis_size("sky")

    def packed(cols):
        return jnp.concatenate([cols[:, : row_count // 2], cols[:, row_count // 2 :]], axis=2)

    spectral, dirty_r, dirty_l = lax.optimization_barrier(
        (spectral, packed(dirty[:, :, slot_width - HALF :]), packed(dirty[:, :, :HALF]))
    )
    model_full = lax.all_gather(model, "chan", axis=1, tiled=True)
    spec_local = lax.dynamic_slice_in_dim(spectral, lax.axis_index("chan") * local_chans, local_chans, 0)
    image = spec_local[:, 0][:, None, None] * model_full[0][None]
    for basis_idx in range(1, basis):
        image = image + spec_local[:, basis_idx][:, None, None] * model_full[basis_idx][None]
    image = image.astype(jnp.bfloat16)
    to_right = jnp.concatenate([image, dirty_r], axis=1)
    to_left = jnp.concatenate([image, dirty_l], axis=1)
    left = from_behind(to_right, "sky", 1)
    right = from_behind(to_left, "sky", -1)

    taps = jnp.concatenate([psf_rows, psf_cols], axis=1)
    taps = jnp.pad(taps, ((0, 0), (0, 0), (0, LANES - TAPS)))
    piece_rows = row_count // chan_count
    ext = slot_width + 2 * HALF
    band_shapes = (
        jax.ShapeDtypeStruct((local_chans, ext, rank_count * slot_width), jnp.bfloat16),
        jax.ShapeDtypeStruct((local_chans, rank_count, row_count, row_count), jnp.bfloat16),
    )
    bands = pl.pallas_call(
        functools.partial(band_kernel, rank_count, local_chans, slot_width),
        out_shape=band_shapes * 2,
        in_specs=[vmem_spec()],
        out_specs=[vmem_spec()] * 4,
    )(taps)
    residual, partial_value = pl.pallas_call(
        functools.partial(main_kernel, rank_count, local_chans, sky_count),
        out_shape=(
            jax.ShapeDtypeStruct(dirty.shape, jnp.bfloat16),
            jax.ShapeDtypeStruct((chan_count, basis, piece_rows, slot_width), jnp.float32),
        ),
        grid=(local_chans,),
        in_specs=[smem_spec()] + [per_chan(a.shape) for a in (*bands, left, image, right, dirty)],
        out_specs=[
            per_chan(dirty.shape),
            pl.BlockSpec((chan_count, basis, piece_rows, slot_width), lambda c: (0, 0, 0, 0)),
        ],
    )(spectral, *bands, left, to_right, right, dirty)

    pieces = lax.all_to_all(partial_value, "chan", 0, 0, tiled=True)

    gram_rows = jnp.einsum("crt,cst->crs", psf_rows, psf_rows, precision=lax.Precision.HIGHEST)
    gram_cols = jnp.einsum("crt,cst->crs", psf_cols, psf_cols, precision=lax.Precision.HIGHEST)
    energy = jnp.sum(gram_rows * gram_cols, axis=(1, 2))
    curvature = jnp.sum(spectral * spectral * energy[:, None], axis=0)
    own_rows = lax.dynamic_slice_in_dim(model_full, lax.axis_index("chan") * piece_rows, piece_rows, 1)
    model_new = own_rows + pieces.sum(0) / curvature[:, None, None]
    return (residual, model_new)


def solution(mesh):
    placed = (P("chan", None, "sky"), P(None, "chan", "sky"), P(), P(), P(), P())
    return jax.shard_map(
        body,
        mesh=mesh,
        in_specs=placed,
        out_specs=(P("chan", None, "sky"), P(None, "chan", "sky")),
        check_vma=False,
    )
```
